32 devices in a mesh: row: 8 (over z, x), col: 4 (over y, core).
Axes of the slice: x: 2, y: 2, z: 4, core: 2. Of those that a mesh axis runs over, the one named last changes fastest.
Arguments:
- amplitudes: bfloat16 [3072, 65536], P('row', 'col'), may hold values from -6 to 6
- integrals: bfloat16 [65536, 1024], P('col', 'row'), may hold values from -0.09375 to 0.09375
- pair_label: int32 [24], P('row'), may hold values from 0 to 7
- orbital_irrep: int32 [256], replicated, may hold values from 0 to 7
- column_label: int32 [8], replicated, may hold values from 0 to 7
Outputs:
- ladder: bfloat16 [1024, 3072], P('col', 'row')
The draws below stay inside these ranges and needn't reach their ends.
Inputs may be any that keep to these rules, and one draw needn't show every extreme that they name: `orbital_irrep`: irrep labels of the window's virtual orbitals.
All inputs are finite; a program needn't handle non-finite values.
Results may differ from the reference program's by a relative error of at most 0.001.
Values may be sent and summed in bfloat16 or wider, within the bound.
No kernel may reach another device: no remote copies, remote signals or barrier semaphores. Data moves between devices by JAX's collectives and lax.ppermute only.
A program may use at most 128 MiB of HBM per device.

```python
import math
import jax
import jax.numpy as jnp
import numpy as np
from jax import lax

CD_ORBITALS = 256
PAIR_BLOCK = 128
AB_PAIRS = 1024
PAIRS = 3072


def place_ends(values, rng, least, high):
    longest = values.shape.index(max(values.shape))
    spots = []
    for shift in (0, 1):
        where = [jax.random.randint(jax.random.fold_in(rng, axis), (), 0, length) for axis, length in enumerate(values.shape)]
        where[longest] = (where[longest] + shift) % values.shape[longest]
        spots.append(tuple(where))
    return values.at[spots[0]].set(least).at[spots[1]].set(high)


def raised(values, key, source, target, shards_of, factor):
    def block_of(axis_at):
        return (jnp.arange(values.shape[axis_at]) // (values.shape[axis_at] // shards_of)).reshape((-1,) + (1,) * (values.ndim - 1 - axis_at))

    first = jax.random.permutation(key, shards_of)[block_of(target)]
    other_side = (block_of(target) + shards_of // 2) % shards_of
    return jnp.where((block_of(source) == first) | (block_of(source) == other_side), factor * values, values)


def block_levels(rng, extent, split, low, top_value):
    loudness = 1.0
    for dim, parts in split:
        steps = jax.random.uniform(jax.random.fold_in(jax.random.fold_in(rng, 6), dim), (parts,), jnp.float32, low / len(split), top_value / len(split))
        loudness = loudness * jnp.repeat(jnp.exp(steps), extent[dim] // parts).reshape((-1,) + (1,) * (len(extent) - 1 - dim))
    return loudness


def rank_bounds(amount, skew):
    weights = [(1 << 20) // math.isqrt(grade ** skew) + 1 for grade in range(1, amount + 1)]
    deviation = 1 + sum(weights) // (1 << 30)
    return np.cumsum(np.array([max(1, weight // deviation) for weight in weights]))


def ranked_ids(rng, dims, number_of, slope):
    table = rank_bounds(number_of, slope)
    pick = jax.random.randint(jax.random.fold_in(rng, 1), dims, 0, int(table[number_of - 1]))
    grade = jnp.searchsorted(jnp.asarray(table, jnp.int32), pick, side="right")
    return jax.random.permutation(jax.random.fold_in(rng, 2), number_of)[grade].astype(jnp.int32)


def gaussian(key, extent, width, bound, split=(), held_as=jnp.bfloat16):
    loudness = block_levels(key, extent, split, -0.22, 0.18) if split else 1.0
    drawn = jax.random.normal(key, extent, jnp.float32) * width * loudness
    return jnp.minimum(jnp.maximum(drawn, -bound), bound).astype(held_as)


def bell_draw_with(rng, extent, width, most, pieces, heavy, dtype=jnp.bfloat16):
    entries = width * jax.random.normal(rng, extent, jnp.float32)
    if pieces:
        entries = entries * block_levels(rng, extent, pieces, -0.22, 0.18)
    return jnp.clip(raised(entries, jax.random.fold_in(rng, 3), *heavy), -most, most).astype(dtype)


def setup_inputs(seed: int = 0) -> dict:
    keys = jax.random.split(jax.random.key(seed), 6)
    return {
        "amplitudes": gaussian(keys[0], (PAIRS, CD_ORBITALS * CD_ORBITALS), 1.0, 6.0, ((0, 8), (1, 4))),
        "integrals": bell_draw_with(keys[1], (CD_ORBITALS * CD_ORBITALS, AB_PAIRS), (CD_ORBITALS * CD_ORBITALS // 8) ** -0.5, 0.09375, ((0, 4), (1, 8)), (0, 1, 8, 2.0)),
        "pair_label": place_ends(ranked_ids(keys[2], (PAIRS // PAIR_BLOCK,), 8, 2), jax.random.fold_in(keys[2], 3), 0, 7).astype(jnp.int32),
        "orbital_irrep": place_ends(ranked_ids(keys[3], (CD_ORBITALS,), 8, 2), jax.random.fold_in(keys[3], 3), 0, 7).astype(jnp.int32),
        "column_label": place_ends(ranked_ids(keys[4], (AB_PAIRS // PAIR_BLOCK,), 8, 2), jax.random.fold_in(keys[4], 3), 0, 7).astype(jnp.int32),
    }


def reference(amplitudes, integrals, pair_label, orbital_irrep, column_label):
    cd_label = jnp.bitwise_xor(orbital_irrep[:, None], orbital_irrep[None, :])
    ab_label = jnp.repeat(column_label, PAIR_BLOCK)
    int_keep = cd_label.reshape(-1)[:, None] == ab_label[None, :]
    int_kept = jnp.where(int_keep, integrals, jnp.zeros_like(integrals)).astype(jnp.float32)
    block_count = PAIRS // PAIR_BLOCK
    amp_blocks = amplitudes.reshape(block_count, PAIR_BLOCK, CD_ORBITALS, CD_ORBITALS)

    def one_block(packed):
        amp_block, block_label = packed
        keep = (cd_label == block_label)[None, :, :]
        amp_kept = jnp.where(keep, amp_block, jnp.zeros_like(amp_block))
        mirror_kept = jnp.transpose(amp_kept, (0, 2, 1))
        differ = amp_kept.astype(jnp.float32) - mirror_kept.astype(jnp.float32)
        differ = differ.reshape(PAIR_BLOCK, CD_ORBITALS * CD_ORBITALS)
        return jnp.dot(differ, int_kept, precision=lax.Precision.HIGHEST, preferred_element_type=jnp.float32)

    blocks = lax.map(one_block, (amp_blocks, pair_label))
    result = blocks.reshape(PAIRS, AB_PAIRS)
    return jnp.transpose(result).astype(jnp.bfloat16)
```

```python
import jax
import jax.numpy as jnp
from jax import lax
from jax.sharding import PartitionSpec as P

PAIR_BLOCK = 128
IRREPS = 8
TIERS = (4, 5, 8)


def make_body(n_row, n_col):
    def body(amplitudes, integrals, pair_label, orbital_irrep, column_label):
        pair_rows, cd_count = amplitudes.shape
        orb_width = orbital_irrep.shape[0]
        c_count = cd_count // orb_width
        ab_count = integrals.shape[1]
        col_i = lax.axis_index("col")
        row_i = lax.axis_index("row")
        c_irrep = lax.dynamic_slice_in_dim(orbital_irrep, col_i * c_count, c_count)
        cd_label = jnp.bitwise_xor(c_irrep[:, None], orbital_irrep[None, :]).reshape(cd_count)
        row_label = jnp.repeat(pair_label, pair_rows // pair_label.shape[0])
        int_cube = integrals.reshape(c_count, orb_width, ab_count)
        swapped = lax.all_to_all(int_cube, "col", split_axis=1, concat_axis=0, tiled=True)
        mirrored = jnp.transpose(swapped, (1, 0, 2)).reshape(cd_count, ab_count)

        def dense(_):
            ab_label = jnp.repeat(column_label, PAIR_BLOCK)
            amp_keep = row_label[:, None] == cd_label[None, :]
            slab_keep = cd_label[:, None] == ab_label[None, :]
            amp_kept = jnp.where(amp_keep, amplitudes, jnp.zeros_like(amplitudes))
            int_slab = lax.all_gather(integrals, "row", axis=1, tiled=True)
            mirror_slab = lax.all_gather(mirrored, "row", axis=1, tiled=True)
            int_kept = jnp.where(slab_keep, int_slab, jnp.zeros_like(int_slab))
            mirror_kept = jnp.where(slab_keep, mirror_slab, jnp.zeros_like(mirror_slab))
            direct = jnp.einsum("ka,pk->ap", int_kept, amp_kept, preferred_element_type=jnp.float32)
            crossed = jnp.einsum("ka,pk->ap", mirror_kept, amp_kept, preferred_element_type=jnp.float32)
            return direct - crossed

        single = ab_count <= PAIR_BLOCK and PAIR_BLOCK % ab_count == 0
        if not single:
            partial = dense(None)
        else:
            block_label = column_label[(jnp.arange(n_row) * ab_count) // PAIR_BLOCK]
            irreps = jnp.arange(IRREPS, dtype=orbital_irrep.dtype)
            per_irrep = jnp.sum(orbital_irrep[:, None] == irreps[None, :], axis=0)
            per_orb = per_irrep[jnp.bitwise_xor(orbital_irrep[:, None], irreps[None, :])]
            per_col = per_orb.reshape(n_col, c_count, IRREPS).sum(axis=1)
            kept = per_col[:, block_label]
            largest = jnp.max(kept)
            own_counts = per_col[col_i][block_label]
            caps = [t * cd_count // 16 for t in TIERS]
            tier = sum((largest > cap).astype(jnp.int32) for cap in caps)

            def compact(cap):
                def run(_):
                    masks = cd_label[None, :] == block_label[:, None]
                    pos = jnp.cumsum(masks.astype(jnp.int32), axis=1) - 1
                    target = jnp.where(masks, pos, cap)
                    src = jnp.broadcast_to(jnp.arange(cd_count, dtype=jnp.int32), masks.shape)
                    lane = jnp.broadcast_to(jnp.arange(n_row, dtype=jnp.int32)[:, None], masks.shape)
                    idx = jnp.zeros((n_row, cap), jnp.int32).at[lane, target].set(src, mode="drop")
                    valid = jnp.arange(cap)[None, :] < own_counts[:, None]
                    own_idx = idx[row_i]
                    own_valid = valid[row_i][:, None]
                    sent = jnp.concatenate(
                        [jnp.take(integrals, own_idx, axis=0), jnp.take(mirrored, own_idx, axis=0)], axis=1
                    )
                    sent = jnp.where(own_valid, sent, jnp.zeros_like(sent))
                    got = lax.all_gather(sent, "row", axis=0, tiled=False)
                    amp_rows = jnp.take(amplitudes.T, idx, axis=0)
                    prod = jnp.einsum("imq,imp->iqp", got, amp_rows, preferred_element_type=jnp.float32)
                    diff = prod[:, :ab_count] - prod[:, ab_count:]
                    keep = row_label[None, :] == block_label[:, None]
                    diff = jnp.where(keep[:, None, :], diff, jnp.zeros_like(diff))
                    return diff.reshape(n_row * ab_count, pair_rows)

                return run

            branches = [compact(cap) for cap in caps] + [dense]
            partial = lax.switch(tier, branches, None)
        summed = lax.psum_scatter(partial, "col", scatter_dimension=0, tiled=True)
        return summed.astype(jnp.bfloat16)

    return body


def solution(mesh):
    placed = (P("row", "col"), P("col", "row"), P("row"), P(), P())
    return jax.shard_map(
        make_body(mesh.shape["row"], mesh.shape["col"]),
        mesh=mesh,
        in_specs=placed,
        out_specs=P("col", "row"),
        check_vma=False,
    )
```

```python
import jax
import jax.numpy as jnp
from jax import lax
from jax.sharding import PartitionSpec as P

PAIR_BLOCK = 128
IRREPS = 8
TIERS = (4, 5, 8)


def make_body(n_row, n_col):
    def body(amplitudes, integrals, pair_label, orbital_irrep, column_label):
        pair_rows, cd_count = amplitudes.shape
        orb_width = orbital_irrep.shape[0]
        c_count = cd_count // orb_width
        ab_count = integrals.shape[1]
        col_i = lax.axis_index("col")
        row_i = lax.axis_index("row")
        c_irrep = lax.dynamic_slice_in_dim(orbital_irrep, col_i * c_count, c_count)
        cd_label = jnp.bitwise_xor(c_irrep[:, None], orbital_irrep[None, :]).reshape(cd_count)
        row_label = jnp.repeat(pair_label, pair_rows // pair_label.shape[0])
        int_cube = integrals.reshape(c_count, orb_width, ab_count)
        swapped = lax.all_to_all(int_cube, "col", split_axis=1, concat_axis=0, tiled=True)
        mirrored = jnp.transpose(swapped, (1, 0, 2)).reshape(cd_count, ab_count)

        def dense(_):
            ab_label = jnp.repeat(column_label, PAIR_BLOCK)
            amp_keep = row_label[:, None] == cd_label[None, :]
            slab_keep = cd_label[:, None] == ab_label[None, :]
            amp_kept = jnp.where(amp_keep, amplitudes, jnp.zeros_like(amplitudes))
            int_slab = lax.all_gather(integrals, "row", axis=1, tiled=True)
            mirror_slab = lax.all_gather(mirrored, "row", axis=1, tiled=True)
            int_kept = jnp.where(slab_keep, int_slab, jnp.zeros_like(int_slab))
            mirror_kept = jnp.where(slab_keep, mirror_slab, jnp.zeros_like(mirror_slab))
            direct = jnp.einsum("ka,pk->ap", int_kept, amp_kept, preferred_element_type=jnp.float32)
            crossed = jnp.einsum("ka,pk->ap", mirror_kept, amp_kept, preferred_element_type=jnp.float32)
            return direct - crossed

        single = ab_count <= PAIR_BLOCK and PAIR_BLOCK % ab_count == 0
        if not single:
            partial = dense(None)
        else:
            block_label = column_label[(jnp.arange(n_row) * ab_count) // PAIR_BLOCK]
            irreps = jnp.arange(IRREPS, dtype=orbital_irrep.dtype)
            per_irrep = jnp.sum(orbital_irrep[:, None] == irreps[None, :], axis=0)
            per_orb = per_irrep[jnp.bitwise_xor(orbital_irrep[:, None], irreps[None, :])]
            per_col = per_orb.reshape(n_col, c_count, IRREPS).sum(axis=1)
            kept = per_col[:, block_label]
            largest = jnp.max(kept)
            own_counts = per_col[col_i][block_label]
            caps = [t * cd_count // 16 for t in TIERS]
            tier = sum((largest > cap).astype(jnp.int32) for cap in caps)

            def compact(cap):
                def run(_):
                    n_pb = pair_label.shape[0]
                    pb = pair_rows // n_pb
                    own_label = block_label[row_i]
                    wanted = jnp.concatenate([own_label[None], pair_label.astype(block_label.dtype)])
                    iota = jnp.arange(cd_count, dtype=jnp.int32)
                    keys = jnp.where(cd_label[None, :] == wanted[:, None], iota[None, :], iota[None, :] + cd_count)
                    order = jnp.sort(keys, axis=1)[:, :cap]
                    order = jnp.where(order >= cd_count, order - cd_count, order)
                    own_valid = (jnp.arange(cap) < own_counts[row_i])[:, None]
                    both = jnp.concatenate([integrals, mirrored], axis=1)
                    sent = jnp.take(both, order[0], axis=0)
                    sent = jnp.where(own_valid, sent, jnp.zeros_like(sent))
                    got = lax.all_gather(sent, "row", axis=0, tiled=False)
                    amp_t = amplitudes.T.reshape(cd_count, n_pb, pb)
                    amp_rows = jnp.stack([jnp.take(amp_t[:, u], order[1 + u], axis=0) for u in range(n_pb)])
                    prod = jnp.einsum("imq,ump->iuqp", got, amp_rows, preferred_element_type=jnp.float32)
                    diff = prod[:, :, :ab_count] - prod[:, :, ab_count:]
                    keep = block_label[:, None] == pair_label[None, :]
                    diff = jnp.where(keep[:, :, None, None], diff, jnp.zeros_like(diff))
                    return jnp.transpose(diff, (0, 2, 1, 3)).reshape(n_row * ab_count, pair_rows)

                return run

            branches = [compact(cap) for cap in caps] + [dense]
            partial = lax.switch(tier, branches, None)
        summed = lax.psum_scatter(partial, "col", scatter_dimension=0, tiled=True)
        return summed.astype(jnp.bfloat16)

    return body


def solution(mesh):
    placed = (P("row", "col"), P("col", "row"), P("row"), P(), P())
    return jax.shard_map(
        make_body(mesh.shape["row"], mesh.shape["col"]),
        mesh=mesh,
        in_specs=placed,
        out_specs=P("col", "row"),
        check_vma=False,
    )
```

```python
import jax
import jax.numpy as jnp
from jax import lax
from jax.sharding import PartitionSpec as P

PAIR_BLOCK = 128
IRREPS = 8
TIERS = (4, 5, 8)


def make_body(n_row, n_col):
    def body(amplitudes, integrals, pair_label, orbital_irrep, column_label):
        pair_rows, cd_count = amplitudes.shape
        orb_width = orbital_irrep.shape[0]
        c_count = cd_count // orb_width
        ab_count = integrals.shape[1]
        col_i = lax.axis_index("col")
        row_i = lax.axis_index("row")
        c_irrep = lax.dynamic_slice_in_dim(orbital_irrep, col_i * c_count, c_count)
        cd_label = jnp.bitwise_xor(c_irrep[:, None], orbital_irrep[None, :]).reshape(cd_count)
        row_label = jnp.repeat(pair_label, pair_rows // pair_label.shape[0])

        def dense(_):
            int_cube = integrals.reshape(c_count, orb_width, ab_count)
            swapped = lax.all_to_all(int_cube, "col", split_axis=1, concat_axis=0, tiled=True)
            mirrored = jnp.transpose(swapped, (1, 0, 2)).reshape(cd_count, ab_count)
            ab_label = jnp.repeat(column_label, PAIR_BLOCK)
            amp_keep = row_label[:, None] == cd_label[None, :]
            slab_keep = cd_label[:, None] == ab_label[None, :]
            amp_kept = jnp.where(amp_keep, amplitudes, jnp.zeros_like(amplitudes))
            int_slab = lax.all_gather(integrals, "row", axis=1, tiled=True)
            mirror_slab = lax.all_gather(mirrored, "row", axis=1, tiled=True)
            int_kept = jnp.where(slab_keep, int_slab, jnp.zeros_like(int_slab))
            mirror_kept = jnp.where(slab_keep, mirror_slab, jnp.zeros_like(mirror_slab))
            direct = jnp.einsum("ka,pk->ap", int_kept, amp_kept, preferred_element_type=jnp.float32)
            crossed = jnp.einsum("ka,pk->ap", mirror_kept, amp_kept, preferred_element_type=jnp.float32)
            return direct - crossed

        single = ab_count <= PAIR_BLOCK and PAIR_BLOCK % ab_count == 0
        if not single:
            partial = dense(None)
        else:
            block_label = column_label[(jnp.arange(n_row) * ab_count) // PAIR_BLOCK]
            irreps = jnp.arange(IRREPS, dtype=orbital_irrep.dtype)
            per_irrep = jnp.sum(orbital_irrep[:, None] == irreps[None, :], axis=0)
            per_orb = per_irrep[jnp.bitwise_xor(orbital_irrep[:, None], irreps[None, :])]
            per_col = per_orb.reshape(n_col, c_count, IRREPS).sum(axis=1)
            kept = per_col[:, block_label]
            largest = jnp.max(kept)
            own_counts = per_col[col_i][block_label]
            caps = [t * cd_count // 16 for t in TIERS]
            tier = sum((largest > cap).astype(jnp.int32) for cap in caps)

            def compact(cap):
                def run(_):
                    n_pb = pair_label.shape[0]
                    pb = pair_rows // n_pb
                    iota = jnp.arange(cd_count, dtype=jnp.int32)

                    def first(masks):
                        keys = jnp.where(masks, iota[None, :], iota[None, :] + cd_count)
                        order = jnp.sort(keys, axis=1)[:, :cap]
                        return jnp.where(order >= cd_count, order - cd_count, order)

                    own_order = first((cd_label == block_label[row_i])[None, :])[0]
                    own_valid = (jnp.arange(cap) < own_counts[row_i])[:, None]
                    sent = jnp.take(integrals, own_order, axis=0)
                    sent = jnp.where(own_valid, sent, jnp.zeros_like(sent))
                    got = lax.all_gather(sent, "row", axis=0, tiled=False)
                    amp_t = amplitudes.T
                    amp_swap = lax.all_to_all(
                        amp_t.reshape(c_count, orb_width, pair_rows), "col", split_axis=1, concat_axis=0, tiled=True
                    )
                    amp_mirror = jnp.transpose(amp_swap, (1, 0, 2)).reshape(cd_count, pair_rows)
                    p_order = first(cd_label[None, :] == pair_label[:, None].astype(cd_label.dtype))
                    both = jnp.concatenate(
                        [amp_t.reshape(cd_count, n_pb, pb), amp_mirror.reshape(cd_count, n_pb, pb)], axis=2
                    )
                    amp_rows = jnp.stack([jnp.take(both[:, u], p_order[u], axis=0) for u in range(n_pb)])
                    prod = jnp.einsum("imq,ump->iuqp", got, amp_rows, preferred_element_type=jnp.float32)
                    diff = prod[..., :pb] - prod[..., pb:]
                    keep = block_label[:, None] == pair_label[None, :]
                    diff = jnp.where(keep[:, :, None, None], diff, jnp.zeros_like(diff))
                    return jnp.transpose(diff, (0, 2, 1, 3)).reshape(n_row * ab_count, pair_rows)

                return run

            branches = [compact(cap) for cap in caps] + [dense]
            partial = lax.switch(tier, branches, None)
        summed = lax.psum_scatter(partial, "col", scatter_dimension=0, tiled=True)
        return summed.astype(jnp.bfloat16)

    return body


def solution(mesh):
    placed = (P("row", "col"), P("col", "row"), P("row"), P(), P())
    return jax.shard_map(
        make_body(mesh.shape["row"], mesh.shape["col"]),
        mesh=mesh,
        in_specs=placed,
        out_specs=P("col", "row"),
        check_vma=False,
    )
```

```python
import jax
import jax.numpy as jnp
from jax import lax
from jax.sharding import PartitionSpec as P

PAIR_BLOCK = 128
IRREPS = 8
TIERS = (4, 5, 8)


def make_body(n_row, n_col):
    def body(amplitudes, integrals, pair_label, orbital_irrep, column_label):
        pair_rows, cd_count = amplitudes.shape
        orb_width = orbital_irrep.shape[0]
        c_count = cd_count // orb_width
        ab_count = integrals.shape[1]
        col_i = lax.axis_index("col")
        row_i = lax.axis_index("row")
        c_irrep = lax.dynamic_slice_in_dim(orbital_irrep, col_i * c_count, c_count)
        cd_label = jnp.bitwise_xor(c_irrep[:, None], orbital_irrep[None, :]).reshape(cd_count)
        row_label = jnp.repeat(pair_label, pair_rows // pair_label.shape[0])

        def dense(_):
            int_cube = integrals.reshape(c_count, orb_width, ab_count)
            swapped = lax.all_to_all(int_cube, "col", split_axis=1, concat_axis=0, tiled=True)
            mirrored = jnp.transpose(swapped, (1, 0, 2)).reshape(cd_count, ab_count)
            ab_label = jnp.repeat(column_label, PAIR_BLOCK)
            amp_keep = row_label[:, None] == cd_label[None, :]
            slab_keep = cd_label[:, None] == ab_label[None, :]
            amp_kept = jnp.where(amp_keep, amplitudes, jnp.zeros_like(amplitudes))
            int_slab = lax.all_gather(integrals, "row", axis=1, tiled=True)
            mirror_slab = lax.all_gather(mirrored, "row", axis=1, tiled=True)
            int_kept = jnp.where(slab_keep, int_slab, jnp.zeros_like(int_slab))
            mirror_kept = jnp.where(slab_keep, mirror_slab, jnp.zeros_like(mirror_slab))
            direct = jnp.einsum("ka,pk->ap", int_kept, amp_kept, preferred_element_type=jnp.float32)
            crossed = jnp.einsum("ka,pk->ap", mirror_kept, amp_kept, preferred_element_type=jnp.float32)
            return direct - crossed

        single = ab_count <= PAIR_BLOCK and PAIR_BLOCK % ab_count == 0
        if not single:
            partial = dense(None)
        else:
            block_label = column_label[(jnp.arange(n_row) * ab_count) // PAIR_BLOCK]
            irreps = jnp.arange(IRREPS, dtype=orbital_irrep.dtype)
            per_irrep = jnp.sum(orbital_irrep[:, None] == irreps[None, :], axis=0)
            per_orb = per_irrep[jnp.bitwise_xor(orbital_irrep[:, None], irreps[None, :])]
            per_col = per_orb.reshape(n_col, c_count, IRREPS).sum(axis=1)
            kept = per_col[:, block_label]
            largest = jnp.max(kept)
            own_counts = per_col[col_i][block_label]
            caps = [t * cd_count // 16 for t in TIERS]
            tier = sum((largest > cap).astype(jnp.int32) for cap in caps)

            def compact(cap):
                def run(_):
                    n_pb = pair_label.shape[0]
                    pb = pair_rows // n_pb
                    iota = jnp.arange(cd_count, dtype=jnp.int32)

                    def first(masks):
                        keys = jnp.where(masks, iota[None, :], iota[None, :] + cd_count)
                        order = jnp.sort(keys, axis=1)[:, :cap]
                        return jnp.where(order >= cd_count, order - cd_count, order)

                    own_order = first((cd_label == block_label[row_i])[None, :])[0]
                    own_valid = (jnp.arange(cap) < own_counts[row_i])[:, None]
                    sent = jnp.take(integrals, own_order, axis=0)
                    sent = jnp.where(own_valid, sent, jnp.zeros_like(sent))
                    got = lax.all_gather(sent, "row", axis=0, tiled=False)
                    amp_dc = jnp.transpose(amplitudes.reshape(pair_rows, c_count, orb_width), (2, 1, 0))
                    amp_dc = amp_dc.reshape(cd_count, pair_rows)
                    received = lax.all_to_all(amp_dc, "col", split_axis=0, concat_axis=0, tiled=True)
                    p_order = first(cd_label[None, :] == pair_label[:, None].astype(cd_label.dtype))
                    c_loc = p_order // orb_width
                    d_all = p_order % orb_width
                    direct_at = d_all * c_count + c_loc
                    mirror_at = ((d_all // c_count) * c_count + c_loc) * c_count + d_all % c_count
                    amp_rows = jnp.stack(
                        [
                            jnp.concatenate(
                                [
                                    jnp.take(amp_dc[:, u * pb:(u + 1) * pb], direct_at[u], axis=0),
                                    jnp.take(received[:, u * pb:(u + 1) * pb], mirror_at[u], axis=0),
                                ],
                                axis=1,
                            )
                            for u in range(n_pb)
                        ]
                    )
                    prod = jnp.einsum("imq,ump->iuqp", got, amp_rows, preferred_element_type=jnp.float32)
                    diff = prod[..., :pb] - prod[..., pb:]
                    keep = block_label[:, None] == pair_label[None, :]
                    diff = jnp.where(keep[:, :, None, None], diff, jnp.zeros_like(diff))
                    return jnp.transpose(diff, (0, 2, 1, 3)).reshape(n_row * ab_count, pair_rows)

                return run

            branches = [compact(cap) for cap in caps] + [dense]
            partial = lax.switch(tier, branches, None)
        summed = lax.psum_scatter(partial, "col", scatter_dimension=0, tiled=True)
        return summed.astype(jnp.bfloat16)

    return body


def solution(mesh):
    placed = (P("row", "col"), P("col", "row"), P("row"), P(), P())
    return jax.shard_map(
        make_body(mesh.shape["row"], mesh.shape["col"]),
        mesh=mesh,
        in_specs=placed,
        out_specs=P("col", "row"),
        check_vma=False,
    )
```

```python
import jax
import jax.numpy as jnp
from jax import lax
from jax.sharding import PartitionSpec as P

PAIR_BLOCK = 128
IRREPS = 8
TIERS = (4, 5, 6, 8)


def make_body(n_row, n_col):
    def body(amplitudes, integrals, pair_label, orbital_irrep, column_label):
        pair_rows, cd_count = amplitudes.shape
        orb_width = orbital_irrep.shape[0]
        c_count = cd_count // orb_width
        ab_count = integrals.shape[1]
        col_i = lax.axis_index("col")
        row_i = lax.axis_index("row")
        c_irrep = lax.dynamic_slice_in_dim(orbital_irrep, col_i * c_count, c_count)
        cd_label = jnp.bitwise_xor(c_irrep[:, None], orbital_irrep[None, :]).reshape(cd_count)
        row_label = jnp.repeat(pair_label, pair_rows // pair_label.shape[0])

        def dense(_):
            int_cube = integrals.reshape(c_count, orb_width, ab_count)
            swapped = lax.all_to_all(int_cube, "col", split_axis=1, concat_axis=0, tiled=True)
            mirrored = jnp.transpose(swapped, (1, 0, 2)).reshape(cd_count, ab_count)
            ab_label = jnp.repeat(column_label, PAIR_BLOCK)
            amp_keep = row_label[:, None] == cd_label[None, :]
            slab_keep = cd_label[:, None] == ab_label[None, :]
            amp_kept = jnp.where(amp_keep, amplitudes, jnp.zeros_like(amplitudes))
            int_slab = lax.all_gather(integrals, "row", axis=1, tiled=True)
            mirror_slab = lax.all_gather(mirrored, "row", axis=1, tiled=True)
            int_kept = jnp.where(slab_keep, int_slab, jnp.zeros_like(int_slab))
            mirror_kept = jnp.where(slab_keep, mirror_slab, jnp.zeros_like(mirror_slab))
            direct = jnp.einsum("ka,pk->ap", int_kept, amp_kept, preferred_element_type=jnp.float32)
            crossed = jnp.einsum("ka,pk->ap", mirror_kept, amp_kept, preferred_element_type=jnp.float32)
            return direct - crossed

        single = ab_count <= PAIR_BLOCK and PAIR_BLOCK % ab_count == 0
        if not single:
            partial = dense(None)
        else:
            block_label = column_label[(jnp.arange(n_row) * ab_count) // PAIR_BLOCK]
            irreps = jnp.arange(IRREPS, dtype=orbital_irrep.dtype)
            blk_irrep = orbital_irrep.reshape(n_col, c_count)
            blk_cnt = jnp.sum(blk_irrep[:, :, None] == irreps[None, None, :], axis=1)
            xor_tab = jnp.bitwise_xor(irreps[:, None], irreps[None, :])
            pair_cnt = jnp.einsum("ak,bkl->abl", blk_cnt, blk_cnt[:, xor_tab])
            largest = jnp.max(pair_cnt[:, :, block_label])
            pair_cells = c_count * c_count
            caps = [t * pair_cells // 16 for t in TIERS]
            tier = sum((largest > cap).astype(jnp.int32) for cap in caps)
            own_irrep = blk_irrep[col_i]
            n_pb = pair_label.shape[0]
            pb = pair_rows // n_pb
            amp_dc = jnp.transpose(amplitudes.reshape(pair_rows, c_count, orb_width), (2, 1, 0))
            amp_dc = amp_dc.reshape(cd_count, pair_rows)

            def first(masks, cap):
                iota = jnp.arange(masks.shape[-1], dtype=jnp.int32)
                keys = jnp.where(masks, iota, iota + masks.shape[-1])
                order = lax.sort(keys, dimension=masks.ndim - 1)[..., :cap]
                valid = order < masks.shape[-1]
                return jnp.where(valid, order, 0), valid

            def compact(cap):
                def run(_):
                    labels = jnp.concatenate([block_label[row_i][None], pair_label.astype(block_label.dtype)])
                    own_lab = jnp.bitwise_xor(own_irrep[:, None, None], blk_irrep[None, :, :])
                    own_lab = jnp.transpose(own_lab, (1, 0, 2)).reshape(n_col, pair_cells)
                    order, valid = first(own_lab[None] == labels[:, None, None], cap)
                    c_loc = order // c_count
                    d_all = jnp.arange(n_col, dtype=jnp.int32)[None, :, None] * c_count + order % c_count
                    sent_at = (c_loc * orb_width + d_all)[0].reshape(n_col * cap)
                    sent = jnp.take(integrals, sent_at, axis=0)
                    sent = jnp.where(valid[0].reshape(n_col * cap, 1), sent, jnp.zeros_like(sent))
                    got = lax.all_gather(sent, "row", axis=0, tiled=False)
                    direct_at = (d_all * c_count + c_loc)[1:]
                    out_lab = jnp.bitwise_xor(blk_irrep[:, :, None], own_irrep[None, None, :]).reshape(n_col, pair_cells)
                    out_order, _ = first(out_lab[None] == labels[1:, None, None], cap)
                    out_at = jnp.arange(n_col, dtype=jnp.int32)[None, :, None] * pair_cells + out_order
                    outgoing = jnp.concatenate(
                        [
                            jnp.take(amp_dc[:, u * pb:(u + 1) * pb], out_at[u].reshape(n_col * cap), axis=0)
                            for u in range(n_pb)
                        ],
                        axis=1,
                    )
                    incoming = lax.all_to_all(outgoing, "col", split_axis=0, concat_axis=0, tiled=True)
                    amp_rows = jnp.stack(
                        [
                            jnp.concatenate(
                                [
                                    jnp.take(amp_dc[:, u * pb:(u + 1) * pb], direct_at[u].reshape(n_col * cap), axis=0),
                                    incoming[:, u * pb:(u + 1) * pb],
                                ],
                                axis=1,
                            )
                            for u in range(n_pb)
                        ]
                    )
                    got = got.reshape(n_row, n_col * cap, ab_count)
                    prod = jnp.einsum("imq,ump->iuqp", got, amp_rows, preferred_element_type=jnp.float32)
                    diff = prod[..., :pb] - prod[..., pb:]
                    keep = block_label[:, None] == pair_label[None, :]
                    diff = jnp.where(keep[:, :, None, None], diff, jnp.zeros_like(diff))
                    return jnp.transpose(diff, (0, 2, 1, 3)).reshape(n_row * ab_count, pair_rows)

                return run

            branches = [compact(cap) for cap in caps] + [dense]
            partial = lax.switch(tier, branches, None)
        summed = lax.psum_scatter(partial, "col", scatter_dimension=0, tiled=True)
        return summed.astype(jnp.bfloat16)

    return body


def solution(mesh):
    placed = (P("row", "col"), P("col", "row"), P("row"), P(), P())
    return jax.shard_map(
        make_body(mesh.shape["row"], mesh.shape["col"]),
        mesh=mesh,
        in_specs=placed,
        out_specs=P("col", "row"),
        check_vma=False,
    )
```

```python
import jax
import jax.numpy as jnp
from jax import lax
from jax.experimental import pallas as pl
from jax.experimental.pallas import tpu as pltpu
from jax.sharding import PartitionSpec as P

PAIR_BLOCK = 128
IRREPS = 8
TIERS = (4, 5, 6, 8)


def _compact_kernel(base_ref, pos_ref, src_ref, out_ref, *, lists, width, span, blocks):
    b = pl.program_id(0)

    @pl.when(b == 0)
    def _():
        out_ref[...] = jnp.zeros_like(out_ref)

    rows = lax.broadcasted_iota(jnp.int32, (span, pos_ref.shape[1]), 0)
    for l in range(lists):
        start = pl.multiple_of(base_ref[l * blocks + b], 16)
        onehot = (rows == pos_ref[l:l + 1, :] - start).astype(src_ref.dtype)
        part = jnp.dot(onehot, src_ref[:, l * width:(l + 1) * width], preferred_element_type=jnp.float32)
        out_ref[l, pl.ds(start, span), :] += part


def compact_rows(source, masks, chunk, cap, lists, width):
    total, _ = source.shape
    chunks = total // chunk
    step = min(512, chunk)
    blocks = total // step
    span = step + 16
    flat = masks.reshape(lists, chunks, chunk).astype(jnp.int32)
    rank = jnp.cumsum(flat, axis=2) - flat
    offset = jnp.arange(chunks, dtype=jnp.int32)[None, :, None] * cap
    pos = jnp.where((flat > 0) & (rank < cap), offset + rank, -1).reshape(lists, total)
    first = (offset + jnp.minimum(rank, cap)).reshape(lists, blocks, step)[:, :, 0]
    base = ((first // 16) * 16).reshape(lists * blocks)
    out = pl.pallas_call(
        lambda *refs: _compact_kernel(*refs, lists=lists, width=width, span=span, blocks=blocks),
        out_shape=jax.ShapeDtypeStruct((lists, chunks * cap + span, width), jnp.float32),
        grid_spec=pltpu.PrefetchScalarGridSpec(
            num_scalar_prefetch=1,
            grid=(blocks,),
            in_specs=[
                pl.BlockSpec((lists, step), lambda b, base: (0, b)),
                pl.BlockSpec((step, lists * width), lambda b, base: (b, 0)),
            ],
            out_specs=pl.BlockSpec((lists, chunks * cap + span, width), lambda b, base: (0, 0, 0)),
        ),
        compiler_params=pltpu.CompilerParams(dimension_semantics=("arbitrary",)),
    )(base, pos, source)
    return out[:, : chunks * cap].astype(source.dtype)


def make_body(n_row, n_col):
    def body(amplitudes, integrals, pair_label, orbital_irrep, column_label):
        pair_rows, cd_count = amplitudes.shape
        orb_width = orbital_irrep.shape[0]
        c_count = cd_count // orb_width
        ab_count = integrals.shape[1]
        col_i = lax.axis_index("col")
        row_i = lax.axis_index("row")
        c_irrep = lax.dynamic_slice_in_dim(orbital_irrep, col_i * c_count, c_count)
        cd_label = jnp.bitwise_xor(c_irrep[:, None], orbital_irrep[None, :]).reshape(cd_count)
        row_label = jnp.repeat(pair_label, pair_rows // pair_label.shape[0])

        def dense(_):
            int_cube = integrals.reshape(c_count, orb_width, ab_count)
            swapped = lax.all_to_all(int_cube, "col", split_axis=1, concat_axis=0, tiled=True)
            mirrored = jnp.transpose(swapped, (1, 0, 2)).reshape(cd_count, ab_count)
            ab_label = jnp.repeat(column_label, PAIR_BLOCK)
            amp_keep = row_label[:, None] == cd_label[None, :]
            slab_keep = cd_label[:, None] == ab_label[None, :]
            amp_kept = jnp.where(amp_keep, amplitudes, jnp.zeros_like(amplitudes))
            int_slab = lax.all_gather(integrals, "row", axis=1, tiled=True)
            mirror_slab = lax.all_gather(mirrored, "row", axis=1, tiled=True)
            int_kept = jnp.where(slab_keep, int_slab, jnp.zeros_like(int_slab))
            mirror_kept = jnp.where(slab_keep, mirror_slab, jnp.zeros_like(mirror_slab))
            direct = jnp.einsum("ka,pk->ap", int_kept, amp_kept, preferred_element_type=jnp.float32)
            crossed = jnp.einsum("ka,pk->ap", mirror_kept, amp_kept, preferred_element_type=jnp.float32)
            return direct - crossed

        single = ab_count <= PAIR_BLOCK and PAIR_BLOCK % ab_count == 0
        if not single:
            partial = dense(None)
        else:
            block_label = column_label[(jnp.arange(n_row) * ab_count) // PAIR_BLOCK]
            irreps = jnp.arange(IRREPS, dtype=orbital_irrep.dtype)
            blk_irrep = orbital_irrep.reshape(n_col, c_count)
            blk_cnt = jnp.sum(blk_irrep[:, :, None] == irreps[None, None, :], axis=1)
            xor_tab = jnp.bitwise_xor(irreps[:, None], irreps[None, :])
            pair_cnt = jnp.einsum("ak,bkl->abl", blk_cnt, blk_cnt[:, xor_tab])
            largest = jnp.max(pair_cnt[:, :, block_label])
            pair_cells = c_count * c_count
            caps = [t * pair_cells // 16 for t in TIERS]
            tier = sum((largest > cap).astype(jnp.int32) for cap in caps)
            own_irrep = blk_irrep[col_i]
            n_pb = pair_label.shape[0]
            pb = pair_rows // n_pb
            amp_dc = jnp.transpose(amplitudes.reshape(pair_rows, c_count, orb_width), (2, 1, 0))
            amp_dc = amp_dc.reshape(cd_count, pair_rows)

            amp_jcd = jnp.transpose(amplitudes.reshape(pair_rows, c_count, n_col, c_count), (2, 1, 3, 0))
            amp_jcd = amp_jcd.reshape(cd_count, pair_rows)
            int_jdc = jnp.transpose(integrals.reshape(c_count, n_col, c_count, ab_count), (1, 2, 0, 3))
            int_jdc = int_jdc.reshape(cd_count, ab_count)
            lab_jdc = jnp.bitwise_xor(blk_irrep[:, :, None], own_irrep[None, None, :])
            lab_bcd = jnp.bitwise_xor(own_irrep[None, :, None], blk_irrep[:, None, :])
            p_lab = pair_label.astype(lab_jdc.dtype)

            def compact(cap):
                def run(_):
                    sent = compact_rows(
                        int_jdc, (lab_jdc == block_label[row_i])[None], pair_cells, cap, 1, ab_count
                    )[0]
                    got = lax.all_gather(sent, "row", axis=0, tiled=False)
                    outgoing = compact_rows(
                        amp_jcd, lab_bcd[None] == p_lab[:, None, None, None], pair_cells, cap, n_pb, pb
                    )
                    outgoing = jnp.transpose(outgoing, (1, 0, 2)).reshape(n_col * cap, n_pb * pb)
                    incoming = lax.all_to_all(outgoing, "col", split_axis=0, concat_axis=0, tiled=True)
                    incoming = jnp.transpose(incoming.reshape(n_col * cap, n_pb, pb), (1, 0, 2))
                    direct = compact_rows(
                        amp_dc, lab_jdc[None] == p_lab[:, None, None, None], pair_cells, cap, n_pb, pb
                    )
                    amp_rows = jnp.concatenate([direct, incoming], axis=2)
                    prod = jnp.einsum("imq,ump->iuqp", got, amp_rows, preferred_element_type=jnp.float32)
                    diff = prod[..., :pb] - prod[..., pb:]
                    keep = block_label[:, None] == pair_label[None, :]
                    diff = jnp.where(keep[:, :, None, None], diff, jnp.zeros_like(diff))
                    return jnp.transpose(diff, (0, 2, 1, 3)).reshape(n_row * ab_count, pair_rows)

                return run

            branches = [compact(cap) for cap in caps] + [dense]
            partial = lax.switch(tier, branches, None)
        summed = lax.psum_scatter(partial, "col", scatter_dimension=0, tiled=True)
        return summed.astype(jnp.bfloat16)

    return body


def solution(mesh):
    placed = (P("row", "col"), P("col", "row"), P("row"), P(), P())
    return jax.shard_map(
        make_body(mesh.shape["row"], mesh.shape["col"]),
        mesh=mesh,
        in_specs=placed,
        out_specs=P("col", "row"),
        check_vma=False,
    )
```

```python
import jax
import jax.numpy as jnp
from jax import lax
from jax.experimental import pallas as pl
from jax.experimental.pallas import tpu as pltpu
from jax.sharding import PartitionSpec as P

PAIR_BLOCK = 128
IRREPS = 8
TIERS = (4, 5, 6, 8)


def _compact_kernel(base_ref, pos_ref, src_ref, out_ref, acc_ref, *, lists, width, sub, subs, steps):
    b = pl.program_id(0)
    span = sub + 16

    @pl.when(b == 0)
    def _():
        acc_ref[...] = jnp.zeros_like(acc_ref)

    rows = lax.broadcasted_iota(jnp.int32, (span, sub), 0)
    for l in range(lists):
        for k in range(subs):
            start = pl.multiple_of(base_ref[(l * steps + b) * subs + k], 16)
            onehot = (rows == pos_ref[l:l + 1, k * sub:(k + 1) * sub] - start).astype(src_ref.dtype)
            part = jnp.dot(
                onehot, src_ref[k * sub:(k + 1) * sub, l * width:(l + 1) * width], preferred_element_type=jnp.float32
            )
            acc_ref[pl.ds(start, span), l * width:(l + 1) * width] += part

    @pl.when(b == steps - 1)
    def _():
        out_ref[...] = acc_ref[: out_ref.shape[0], :].astype(out_ref.dtype)


def compact_rows(source, masks, chunk, cap, lists, width):
    total, _ = source.shape
    chunks = total // chunk
    sub = min(128, chunk)
    step = min(512, chunk)
    steps = total // step
    flat = masks.reshape(lists, chunks, chunk).astype(jnp.int32)
    rank = jnp.cumsum(flat, axis=2) - flat
    offset = jnp.arange(chunks, dtype=jnp.int32)[None, :, None] * cap
    pos = jnp.where((flat > 0) & (rank < cap), offset + rank, -1).reshape(lists, total)
    first = (offset + jnp.minimum(rank, cap)).reshape(lists, total // sub, sub)[:, :, 0]
    base = ((first // 16) * 16).reshape(lists * (total // sub))
    kept = chunks * cap
    return pl.pallas_call(
        lambda *refs: _compact_kernel(*refs, lists=lists, width=width, sub=sub, subs=step // sub, steps=steps),
        out_shape=jax.ShapeDtypeStruct((kept, lists * width), source.dtype),
        grid_spec=pltpu.PrefetchScalarGridSpec(
            num_scalar_prefetch=1,
            grid=(steps,),
            in_specs=[
                pl.BlockSpec((lists, step), lambda b, base: (0, b)),
                pl.BlockSpec((step, lists * width), lambda b, base: (b, 0)),
            ],
            out_specs=pl.BlockSpec((kept, lists * width), lambda b, base: (0, 0)),
            scratch_shapes=[pltpu.VMEM((kept + sub + 16, lists * width), jnp.float32)],
        ),
        compiler_params=pltpu.CompilerParams(dimension_semantics=("arbitrary",)),
    )(base, pos, source)


def make_body(n_row, n_col):
    def body(amplitudes, integrals, pair_label, orbital_irrep, column_label):
        pair_rows, cd_count = amplitudes.shape
        orb_width = orbital_irrep.shape[0]
        c_count = cd_count // orb_width
        ab_count = integrals.shape[1]
        col_i = lax.axis_index("col")
        row_i = lax.axis_index("row")
        c_irrep = lax.dynamic_slice_in_dim(orbital_irrep, col_i * c_count, c_count)
        cd_label = jnp.bitwise_xor(c_irrep[:, None], orbital_irrep[None, :]).reshape(cd_count)
        row_label = jnp.repeat(pair_label, pair_rows // pair_label.shape[0])

        def dense(_):
            int_cube = integrals.reshape(c_count, orb_width, ab_count)
            swapped = lax.all_to_all(int_cube, "col", split_axis=1, concat_axis=0, tiled=True)
            mirrored = jnp.transpose(swapped, (1, 0, 2)).reshape(cd_count, ab_count)
            ab_label = jnp.repeat(column_label, PAIR_BLOCK)
            amp_keep = row_label[:, None] == cd_label[None, :]
            slab_keep = cd_label[:, None] == ab_label[None, :]
            amp_kept = jnp.where(amp_keep, amplitudes, jnp.zeros_like(amplitudes))
            int_slab = lax.all_gather(integrals, "row", axis=1, tiled=True)
            mirror_slab = lax.all_gather(mirrored, "row", axis=1, tiled=True)
            int_kept = jnp.where(slab_keep, int_slab, jnp.zeros_like(int_slab))
            mirror_kept = jnp.where(slab_keep, mirror_slab, jnp.zeros_like(mirror_slab))
            direct = jnp.einsum("ka,pk->ap", int_kept, amp_kept, preferred_element_type=jnp.float32)
            crossed = jnp.einsum("ka,pk->ap", mirror_kept, amp_kept, preferred_element_type=jnp.float32)
            return direct - crossed

        single = ab_count <= PAIR_BLOCK and PAIR_BLOCK % ab_count == 0
        if not single:
            partial = dense(None)
        else:
            block_label = column_label[(jnp.arange(n_row) * ab_count) // PAIR_BLOCK]
            irreps = jnp.arange(IRREPS, dtype=orbital_irrep.dtype)
            blk_irrep = orbital_irrep.reshape(n_col, c_count)
            blk_cnt = jnp.sum(blk_irrep[:, :, None] == irreps[None, None, :], axis=1)
            xor_tab = jnp.bitwise_xor(irreps[:, None], irreps[None, :])
            pair_cnt = jnp.einsum("ak,bkl->abl", blk_cnt, blk_cnt[:, xor_tab])
            largest = jnp.max(pair_cnt[:, :, block_label])
            pair_cells = c_count * c_count
            caps = [t * pair_cells // 16 for t in TIERS]
            tier = sum((largest > cap).astype(jnp.int32) for cap in caps)
            own_irrep = blk_irrep[col_i]
            n_pb = pair_label.shape[0]
            pb = pair_rows // n_pb
            amp_dc = jnp.transpose(amplitudes.reshape(pair_rows, c_count, orb_width), (2, 1, 0))
            amp_dc = amp_dc.reshape(cd_count, pair_rows)

            amp_jcd = jnp.transpose(amplitudes.reshape(pair_rows, c_count, n_col, c_count), (2, 1, 3, 0))
            amp_jcd = amp_jcd.reshape(cd_count, pair_rows)
            int_jdc = jnp.transpose(integrals.reshape(c_count, n_col, c_count, ab_count), (1, 2, 0, 3))
            int_jdc = int_jdc.reshape(cd_count, ab_count)
            lab_jdc = jnp.bitwise_xor(blk_irrep[:, :, None], own_irrep[None, None, :])
            lab_bcd = jnp.bitwise_xor(own_irrep[None, :, None], blk_irrep[:, None, :])
            p_lab = pair_label.astype(lab_jdc.dtype)

            def compact(cap):
                def run(_):
                    sent = compact_rows(
                        int_jdc, (lab_jdc == block_label[row_i])[None], pair_cells, cap, 1, ab_count
                    )
                    got = lax.all_gather(sent, "row", axis=0, tiled=False)
                    outgoing = compact_rows(
                        amp_jcd, lab_bcd[None] == p_lab[:, None, None, None], pair_cells, cap, n_pb, pb
                    )
                    incoming = lax.all_to_all(outgoing, "col", split_axis=0, concat_axis=0, tiled=True)
                    direct = compact_rows(
                        amp_dc, lab_jdc[None] == p_lab[:, None, None, None], pair_cells, cap, n_pb, pb
                    )
                    both = jnp.concatenate([direct, incoming], axis=1)
                    prod = jnp.einsum("imq,mx->iqx", got, both, preferred_element_type=jnp.float32)
                    diff = prod[..., :pair_rows] - prod[..., pair_rows:]
                    keep = block_label[:, None] == row_label[None, :]
                    diff = jnp.where(keep[:, None, :], diff, jnp.zeros_like(diff))
                    return diff.reshape(n_row * ab_count, pair_rows)

                return run

            branches = [compact(cap) for cap in caps] + [dense]
            partial = lax.switch(tier, branches, None)
        summed = lax.psum_scatter(partial, "col", scatter_dimension=0, tiled=True)
        return summed.astype(jnp.bfloat16)

    return body


def solution(mesh):
    placed = (P("row", "col"), P("col", "row"), P("row"), P(), P())
    return jax.shard_map(
        make_body(mesh.shape["row"], mesh.shape["col"]),
        mesh=mesh,
        in_specs=placed,
        out_specs=P("col", "row"),
        check_vma=False,
    )
```

```python
import jax
import jax.numpy as jnp
from jax import lax
from jax.experimental import pallas as pl
from jax.experimental.pallas import tpu as pltpu
from jax.sharding import PartitionSpec as P

PAIR_BLOCK = 128
IRREPS = 8
TIERS = (4, 5, 6, 8)


def _compact_kernel(base_ref, pos_ref, src_ref, out_ref, acc_ref, *, lists, width, sub, subs, steps):
    b = pl.program_id(0)
    span = sub + 16

    @pl.when(b == 0)
    def _():
        acc_ref[...] = jnp.zeros_like(acc_ref)

    rows = lax.broadcasted_iota(jnp.int32, (span, sub), 0)
    for l in range(lists):
        for k in range(subs):
            start = pl.multiple_of(base_ref[(l * steps + b) * subs + k], 16)
            onehot = (rows == pos_ref[l:l + 1, k * sub:(k + 1) * sub] - start).astype(src_ref.dtype)
            part = jnp.dot(
                onehot, src_ref[k * sub:(k + 1) * sub, l * width:(l + 1) * width], preferred_element_type=jnp.float32
            )
            acc_ref[pl.ds(start, span), l * width:(l + 1) * width] += part

    @pl.when(b == steps - 1)
    def _():
        out_ref[...] = acc_ref[: out_ref.shape[0], :].astype(out_ref.dtype)


def compact_rows(source, masks, chunk, cap, lists, width):
    total, _ = source.shape
    chunks = total // chunk
    sub = min(128, chunk)
    step = min(2048, chunk)
    steps = total // step
    flat = masks.reshape(lists, chunks, chunk).astype(jnp.int32)
    rank = jnp.cumsum(flat, axis=2) - flat
    offset = jnp.arange(chunks, dtype=jnp.int32)[None, :, None] * cap
    pos = jnp.where((flat > 0) & (rank < cap), offset + rank, -1).reshape(lists, total)
    first = (offset + jnp.minimum(rank, cap)).reshape(lists, total // sub, sub)[:, :, 0]
    base = ((first // 16) * 16).reshape(lists * (total // sub))
    kept = chunks * cap
    return pl.pallas_call(
        lambda *refs: _compact_kernel(*refs, lists=lists, width=width, sub=sub, subs=step // sub, steps=steps),
        out_shape=jax.ShapeDtypeStruct((kept, lists * width), source.dtype),
        grid_spec=pltpu.PrefetchScalarGridSpec(
            num_scalar_prefetch=1,
            grid=(steps,),
            in_specs=[
                pl.BlockSpec((lists, step), lambda b, base: (0, b)),
                pl.BlockSpec((step, lists * width), lambda b, base: (b, 0)),
            ],
            out_specs=pl.BlockSpec((kept, lists * width), lambda b, base: (0, 0)),
            scratch_shapes=[pltpu.VMEM((kept + sub + 16, lists * width), jnp.float32)],
        ),
        compiler_params=pltpu.CompilerParams(dimension_semantics=("arbitrary",)),
    )(base, pos, source)


def make_body(n_row, n_col):
    def body(amplitudes, integrals, pair_label, orbital_irrep, column_label):
        pair_rows, cd_count = amplitudes.shape
        orb_width = orbital_irrep.shape[0]
        c_count = cd_count // orb_width
        ab_count = integrals.shape[1]
        col_i = lax.axis_index("col")
        row_i = lax.axis_index("row")
        c_irrep = lax.dynamic_slice_in_dim(orbital_irrep, col_i * c_count, c_count)
        cd_label = jnp.bitwise_xor(c_irrep[:, None], orbital_irrep[None, :]).reshape(cd_count)
        row_label = jnp.repeat(pair_label, pair_rows // pair_label.shape[0])

        def dense(_):
            int_cube = integrals.reshape(c_count, orb_width, ab_count)
            swapped = lax.all_to_all(int_cube, "col", split_axis=1, concat_axis=0, tiled=True)
            mirrored = jnp.transpose(swapped, (1, 0, 2)).reshape(cd_count, ab_count)
            ab_label = jnp.repeat(column_label, PAIR_BLOCK)
            amp_keep = row_label[:, None] == cd_label[None, :]
            slab_keep = cd_label[:, None] == ab_label[None, :]
            amp_kept = jnp.where(amp_keep, amplitudes, jnp.zeros_like(amplitudes))
            int_slab = lax.all_gather(integrals, "row", axis=1, tiled=True)
            mirror_slab = lax.all_gather(mirrored, "row", axis=1, tiled=True)
            int_kept = jnp.where(slab_keep, int_slab, jnp.zeros_like(int_slab))
            mirror_kept = jnp.where(slab_keep, mirror_slab, jnp.zeros_like(mirror_slab))
            direct = jnp.einsum("ka,pk->ap", int_kept, amp_kept, preferred_element_type=jnp.float32)
            crossed = jnp.einsum("ka,pk->ap", mirror_kept, amp_kept, preferred_element_type=jnp.float32)
            return direct - crossed

        single = ab_count <= PAIR_BLOCK and PAIR_BLOCK % ab_count == 0
        if not single:
            partial = dense(None)
        else:
            block_label = column_label[(jnp.arange(n_row) * ab_count) // PAIR_BLOCK]
            irreps = jnp.arange(IRREPS, dtype=orbital_irrep.dtype)
            blk_irrep = orbital_irrep.reshape(n_col, c_count)
            blk_cnt = jnp.sum(blk_irrep[:, :, None] == irreps[None, None, :], axis=1)
            xor_tab = jnp.bitwise_xor(irreps[:, None], irreps[None, :])
            pair_cnt = jnp.einsum("ak,bkl->abl", blk_cnt, blk_cnt[:, xor_tab])
            largest = jnp.max(pair_cnt[:, :, block_label])
            pair_cells = c_count * c_count
            caps = [t * pair_cells // 16 for t in TIERS]
            tier = sum((largest > cap).astype(jnp.int32) for cap in caps)
            own_irrep = blk_irrep[col_i]
            n_pb = pair_label.shape[0]
            pb = pair_rows // n_pb

            lab_jdc = jnp.bitwise_xor(blk_irrep[:, :, None], own_irrep[None, None, :])
            lab_bcd = jnp.bitwise_xor(own_irrep[None, :, None], blk_irrep[:, None, :])
            p_lab = pair_label.astype(lab_jdc.dtype)

            def compact(cap):
                def run(_):
                    int_jdc = jnp.transpose(integrals.reshape(c_count, n_col, c_count, ab_count), (1, 2, 0, 3))
                    int_jdc = int_jdc.reshape(cd_count, ab_count)
                    sent = compact_rows(
                        int_jdc, (lab_jdc == block_label[row_i])[None], pair_cells, cap, 1, ab_count
                    )
                    got = lax.all_gather(sent, "row", axis=0, tiled=False)
                    amp_jcd = jnp.transpose(amplitudes.reshape(pair_rows, c_count, n_col, c_count), (2, 1, 3, 0))
                    amp_jcd = amp_jcd.reshape(cd_count, pair_rows)
                    amp_dc = jnp.transpose(amplitudes.reshape(pair_rows, c_count, orb_width), (2, 1, 0))
                    amp_dc = amp_dc.reshape(cd_count, pair_rows)
                    outgoing = compact_rows(
                        amp_jcd, lab_bcd[None] == p_lab[:, None, None, None], pair_cells, cap, n_pb, pb
                    )
                    incoming = lax.all_to_all(outgoing, "col", split_axis=0, concat_axis=0, tiled=True)
                    direct = compact_rows(
                        amp_dc, lab_jdc[None] == p_lab[:, None, None, None], pair_cells, cap, n_pb, pb
                    )
                    both = jnp.concatenate([direct, incoming], axis=1)
                    prod = jnp.einsum("imq,mx->iqx", got, both, preferred_element_type=jnp.float32)
                    diff = prod[..., :pair_rows] - prod[..., pair_rows:]
                    keep = block_label[:, None] == row_label[None, :]
                    diff = jnp.where(keep[:, None, :], diff, jnp.zeros_like(diff))
                    return diff.reshape(n_row * ab_count, pair_rows)

                return run

            branches = [compact(cap) for cap in caps] + [dense]
            partial = lax.switch(tier, branches, None)
        summed = lax.psum_scatter(partial, "col", scatter_dimension=0, tiled=True)
        return summed.astype(jnp.bfloat16)

    return body


def solution(mesh):
    placed = (P("row", "col"), P("col", "row"), P("row"), P(), P())
    return jax.shard_map(
        make_body(mesh.shape["row"], mesh.shape["col"]),
        mesh=mesh,
        in_specs=placed,
        out_specs=P("col", "row"),
        check_vma=False,
    )
```

```python
import jax
import jax.numpy as jnp
from jax import lax
from jax.experimental import pallas as pl
from jax.experimental.pallas import tpu as pltpu
from jax.sharding import PartitionSpec as P

PAIR_BLOCK = 128
IRREPS = 8
TIERS = (4, 5, 6, 8)


def _compact_kernel(base_ref, pos_ref, src_ref, out_ref, acc_ref, *, lists, width, sub, subs, steps):
    b = pl.program_id(0)
    span = sub + 16

    @pl.when(b == 0)
    def _():
        acc_ref[...] = jnp.zeros_like(acc_ref)

    rows = lax.broadcasted_iota(jnp.int32, (span, sub), 0)

    def one(k, carry):
        at = pl.multiple_of(k * sub, sub)
        for l in range(lists):
            start = pl.multiple_of(base_ref[(l * steps + b) * subs + k], 16)
            onehot = (rows == pos_ref[pl.ds(l, 1), pl.ds(at, sub)] - start).astype(src_ref.dtype)
            part = jnp.dot(
                onehot, src_ref[pl.ds(at, sub), l * width:(l + 1) * width], preferred_element_type=jnp.float32
            )
            acc_ref[pl.ds(start, span), l * width:(l + 1) * width] += part
        return carry

    lax.fori_loop(0, subs, one, 0)

    @pl.when(b == steps - 1)
    def _():
        out_ref[...] = acc_ref[: out_ref.shape[0], :].astype(out_ref.dtype)


def compact_rows(source, masks, chunk, cap, lists, width):
    total, _ = source.shape
    chunks = total // chunk
    sub = min(128, chunk)
    step = min(2048, chunk)
    steps = total // step
    flat = masks.reshape(lists, chunks, chunk).astype(jnp.int32)
    rank = jnp.cumsum(flat, axis=2) - flat
    offset = jnp.arange(chunks, dtype=jnp.int32)[None, :, None] * cap
    pos = jnp.where((flat > 0) & (rank < cap), offset + rank, -1).reshape(lists, total)
    first = (offset + jnp.minimum(rank, cap)).reshape(lists, total // sub, sub)[:, :, 0]
    base = ((first // 16) * 16).reshape(lists * (total // sub))
    kept = chunks * cap
    return pl.pallas_call(
        lambda *refs: _compact_kernel(*refs, lists=lists, width=width, sub=sub, subs=step // sub, steps=steps),
        out_shape=jax.ShapeDtypeStruct((kept, lists * width), source.dtype),
        grid_spec=pltpu.PrefetchScalarGridSpec(
            num_scalar_prefetch=1,
            grid=(steps,),
            in_specs=[
                pl.BlockSpec((lists, step), lambda b, base: (0, b)),
                pl.BlockSpec((step, lists * width), lambda b, base: (b, 0)),
            ],
            out_specs=pl.BlockSpec((kept, lists * width), lambda b, base: (0, 0)),
            scratch_shapes=[pltpu.VMEM((kept + sub + 16, lists * width), jnp.float32)],
        ),
        compiler_params=pltpu.CompilerParams(dimension_semantics=("arbitrary",)),
    )(base, pos, source)


def make_body(n_row, n_col):
    def body(amplitudes, integrals, pair_label, orbital_irrep, column_label):
        pair_rows, cd_count = amplitudes.shape
        orb_width = orbital_irrep.shape[0]
        c_count = cd_count // orb_width
        ab_count = integrals.shape[1]
        col_i = lax.axis_index("col")
        row_i = lax.axis_index("row")
        c_irrep = lax.dynamic_slice_in_dim(orbital_irrep, col_i * c_count, c_count)
        cd_label = jnp.bitwise_xor(c_irrep[:, None], orbital_irrep[None, :]).reshape(cd_count)
        row_label = jnp.repeat(pair_label, pair_rows // pair_label.shape[0])

        def dense(_):
            int_cube = integrals.reshape(c_count, orb_width, ab_count)
            swapped = lax.all_to_all(int_cube, "col", split_axis=1, concat_axis=0, tiled=True)
            mirrored = jnp.transpose(swapped, (1, 0, 2)).reshape(cd_count, ab_count)
            ab_label = jnp.repeat(column_label, PAIR_BLOCK)
            amp_keep = row_label[:, None] == cd_label[None, :]
            slab_keep = cd_label[:, None] == ab_label[None, :]
            amp_kept = jnp.where(amp_keep, amplitudes, jnp.zeros_like(amplitudes))
            int_slab = lax.all_gather(integrals, "row", axis=1, tiled=True)
            mirror_slab = lax.all_gather(mirrored, "row", axis=1, tiled=True)
            int_kept = jnp.where(slab_keep, int_slab, jnp.zeros_like(int_slab))
            mirror_kept = jnp.where(slab_keep, mirror_slab, jnp.zeros_like(mirror_slab))
            direct = jnp.einsum("ka,pk->ap", int_kept, amp_kept, preferred_element_type=jnp.float32)
            crossed = jnp.einsum("ka,pk->ap", mirror_kept, amp_kept, preferred_element_type=jnp.float32)
            return direct - crossed

        single = ab_count <= PAIR_BLOCK and PAIR_BLOCK % ab_count == 0
        if not single:
            partial = dense(None)
        else:
            block_label = column_label[(jnp.arange(n_row) * ab_count) // PAIR_BLOCK]
            irreps = jnp.arange(IRREPS, dtype=orbital_irrep.dtype)
            blk_irrep = orbital_irrep.reshape(n_col, c_count)
            blk_cnt = jnp.sum(blk_irrep[:, :, None] == irreps[None, None, :], axis=1)
            xor_tab = jnp.bitwise_xor(irreps[:, None], irreps[None, :])
            pair_cnt = jnp.einsum("ak,bkl->abl", blk_cnt, blk_cnt[:, xor_tab])
            largest = jnp.max(pair_cnt[:, :, block_label])
            pair_cells = c_count * c_count
            caps = [t * pair_cells // 16 for t in TIERS]
            tier = sum((largest > cap).astype(jnp.int32) for cap in caps)
            own_irrep = blk_irrep[col_i]
            n_pb = pair_label.shape[0]
            pb = pair_rows // n_pb

            lab_jdc = jnp.bitwise_xor(blk_irrep[:, :, None], own_irrep[None, None, :])
            lab_bcd = jnp.bitwise_xor(own_irrep[None, :, None], blk_irrep[:, None, :])
            p_lab = pair_label.astype(lab_jdc.dtype)

            def compact(cap):
                def run(_):
                    int_jdc = jnp.transpose(integrals.reshape(c_count, n_col, c_count, ab_count), (1, 2, 0, 3))
                    int_jdc = int_jdc.reshape(cd_count, ab_count)
                    sent = compact_rows(
                        int_jdc, (lab_jdc == block_label[row_i])[None], pair_cells, cap, 1, ab_count
                    )
                    got = lax.all_gather(sent, "row", axis=0, tiled=False)
                    amp_jcd = jnp.transpose(amplitudes.reshape(pair_rows, c_count, n_col, c_count), (2, 1, 3, 0))
                    amp_jcd = amp_jcd.reshape(cd_count, pair_rows)
                    amp_dc = jnp.transpose(amplitudes.reshape(pair_rows, c_count, orb_width), (2, 1, 0))
                    amp_dc = amp_dc.reshape(cd_count, pair_rows)
                    outgoing = compact_rows(
                        amp_jcd, lab_bcd[None] == p_lab[:, None, None, None], pair_cells, cap, n_pb, pb
                    )
                    incoming = lax.all_to_all(outgoing, "col", split_axis=0, concat_axis=0, tiled=True)
                    direct = compact_rows(
                        amp_dc, lab_jdc[None] == p_lab[:, None, None, None], pair_cells, cap, n_pb, pb
                    )
                    both = jnp.concatenate([direct, incoming], axis=1)
                    prod = jnp.einsum("imq,mx->iqx", got, both, preferred_element_type=jnp.float32)
                    diff = prod[..., :pair_rows] - prod[..., pair_rows:]
                    keep = block_label[:, None] == row_label[None, :]
                    diff = jnp.where(keep[:, None, :], diff, jnp.zeros_like(diff))
                    return diff.reshape(n_row * ab_count, pair_rows)

                return run

            branches = [compact(cap) for cap in caps] + [dense]
            partial = lax.switch(tier, branches, None)
        parts = lax.all_to_all(
            partial.reshape(n_col, partial.shape[0] // n_col, pair_rows), "col", split_axis=0, concat_axis=0, tiled=True
        )
        return jnp.sum(parts, axis=0).astype(jnp.bfloat16)

    return body


def solution(mesh):
    placed = (P("row", "col"), P("col", "row"), P("row"), P(), P())
    return jax.shard_map(
        make_body(mesh.shape["row"], mesh.shape["col"]),
        mesh=mesh,
        in_specs=placed,
        out_specs=P("col", "row"),
        check_vma=False,
    )
```

```python
import jax
import jax.numpy as jnp
from jax import lax
from jax.experimental import pallas as pl
from jax.experimental.pallas import tpu as pltpu
from jax.sharding import PartitionSpec as P

PAIR_BLOCK = 128
IRREPS = 8
TIERS = (4, 5, 6, 8)


def _compact_kernel(base_ref, pos_ref, src_ref, out_ref, acc_ref, *, lists, width, sub, subs, steps):
    b = pl.program_id(0)
    span = sub + 16

    @pl.when(b == 0)
    def _():
        acc_ref[...] = jnp.zeros_like(acc_ref)

    rows = lax.broadcasted_iota(jnp.int32, (span, sub), 0)
    for l in range(lists):
        for k in range(subs):
            start = pl.multiple_of(base_ref[(l * steps + b) * subs + k], 16)
            onehot = (rows == pos_ref[l:l + 1, k * sub:(k + 1) * sub] - start).astype(src_ref.dtype)
            part = jnp.dot(
                onehot, src_ref[k * sub:(k + 1) * sub, l * width:(l + 1) * width], preferred_element_type=jnp.float32
            )
            acc_ref[pl.ds(start, span), l * width:(l + 1) * width] += part

    @pl.when(b == steps - 1)
    def _():
        out_ref[...] = acc_ref[: out_ref.shape[0], :].astype(out_ref.dtype)


def compact_rows(source, masks, chunk, cap, lists, width):
    total, _ = source.shape
    chunks = total // chunk
    sub = min(128, chunk)
    step = min(2048, chunk)
    steps = total // step
    flat = masks.reshape(lists, chunks, chunk).astype(jnp.int32)
    rank = jnp.cumsum(flat, axis=2) - flat
    offset = jnp.arange(chunks, dtype=jnp.int32)[None, :, None] * cap
    pos = jnp.where((flat > 0) & (rank < cap), offset + rank, -1).reshape(lists, total)
    first = (offset + jnp.minimum(rank, cap)).reshape(lists, total // sub, sub)[:, :, 0]
    base = ((first // 16) * 16).reshape(lists * (total // sub))
    kept = chunks * cap
    return pl.pallas_call(
        lambda *refs: _compact_kernel(*refs, lists=lists, width=width, sub=sub, subs=step // sub, steps=steps),
        out_shape=jax.ShapeDtypeStruct((kept, lists * width), source.dtype),
        grid_spec=pltpu.PrefetchScalarGridSpec(
            num_scalar_prefetch=1,
            grid=(steps,),
            in_specs=[
                pl.BlockSpec((lists, step), lambda b, base: (0, b)),
                pl.BlockSpec((step, lists * width), lambda b, base: (b, 0)),
            ],
            out_specs=pl.BlockSpec((kept, lists * width), lambda b, base: (0, 0)),
            scratch_shapes=[pltpu.VMEM((kept + sub + 16, lists * width), jnp.float32)],
        ),
        compiler_params=pltpu.CompilerParams(dimension_semantics=("arbitrary",)),
    )(base, pos, source)


def _ladder_kernel(match_ref, got_ref, both_ref, out_ref, *, n_pb, pb):
    i = pl.program_id(0)
    half = n_pb * pb
    for u in range(n_pb):

        @pl.when(match_ref[i * n_pb + u] != 0)
        def _():
            g = got_ref[0]
            direct = jnp.dot(g, both_ref[:, u * pb:(u + 1) * pb], preferred_element_type=jnp.float32)
            crossed = jnp.dot(g, both_ref[:, half + u * pb:half + (u + 1) * pb], preferred_element_type=jnp.float32)
            out_ref[0, :, u * pb:(u + 1) * pb] = direct - crossed

        @pl.when(match_ref[i * n_pb + u] == 0)
        def _():
            out_ref[0, :, u * pb:(u + 1) * pb] = jnp.zeros((out_ref.shape[1], pb), out_ref.dtype)


def ladder_blocks(match, got_t, both, n_pb, pb):
    n_blk, ab, rows = got_t.shape
    return pl.pallas_call(
        lambda *refs: _ladder_kernel(*refs, n_pb=n_pb, pb=pb),
        out_shape=jax.ShapeDtypeStruct((n_blk, ab, n_pb * pb), jnp.float32),
        grid_spec=pltpu.PrefetchScalarGridSpec(
            num_scalar_prefetch=1,
            grid=(n_blk,),
            in_specs=[
                pl.BlockSpec((1, ab, rows), lambda i, m: (i, 0, 0)),
                pl.BlockSpec((rows, 2 * n_pb * pb), lambda i, m: (0, 0)),
            ],
            out_specs=pl.BlockSpec((1, ab, n_pb * pb), lambda i, m: (i, 0, 0)),
        ),
        compiler_params=pltpu.CompilerParams(dimension_semantics=("arbitrary",), vmem_limit_bytes=60 * 1024 * 1024),
    )(match, got_t, both)


def make_body(n_row, n_col):
    def body(amplitudes, integrals, pair_label, orbital_irrep, column_label):
        pair_rows, cd_count = amplitudes.shape
        orb_width = orbital_irrep.shape[0]
        c_count = cd_count // orb_width
        ab_count = integrals.shape[1]
        col_i = lax.axis_index("col")
        row_i = lax.axis_index("row")
        c_irrep = lax.dynamic_slice_in_dim(orbital_irrep, col_i * c_count, c_count)
        cd_label = jnp.bitwise_xor(c_irrep[:, None], orbital_irrep[None, :]).reshape(cd_count)
        row_label = jnp.repeat(pair_label, pair_rows // pair_label.shape[0])

        def dense(_):
            int_cube = integrals.reshape(c_count, orb_width, ab_count)
            swapped = lax.all_to_all(int_cube, "col", split_axis=1, concat_axis=0, tiled=True)
            mirrored = jnp.transpose(swapped, (1, 0, 2)).reshape(cd_count, ab_count)
            ab_label = jnp.repeat(column_label, PAIR_BLOCK)
            amp_keep = row_label[:, None] == cd_label[None, :]
            slab_keep = cd_label[:, None] == ab_label[None, :]
            amp_kept = jnp.where(amp_keep, amplitudes, jnp.zeros_like(amplitudes))
            int_slab = lax.all_gather(integrals, "row", axis=1, tiled=True)
            mirror_slab = lax.all_gather(mirrored, "row", axis=1, tiled=True)
            int_kept = jnp.where(slab_keep, int_slab, jnp.zeros_like(int_slab))
            mirror_kept = jnp.where(slab_keep, mirror_slab, jnp.zeros_like(mirror_slab))
            direct = jnp.einsum("ka,pk->ap", int_kept, amp_kept, preferred_element_type=jnp.float32)
            crossed = jnp.einsum("ka,pk->ap", mirror_kept, amp_kept, preferred_element_type=jnp.float32)
            return direct - crossed

        single = ab_count <= PAIR_BLOCK and PAIR_BLOCK % ab_count == 0
        if not single:
            partial = dense(None)
        else:
            block_label = column_label[(jnp.arange(n_row) * ab_count) // PAIR_BLOCK]
            irreps = jnp.arange(IRREPS, dtype=orbital_irrep.dtype)
            blk_irrep = orbital_irrep.reshape(n_col, c_count)
            blk_cnt = jnp.sum(blk_irrep[:, :, None] == irreps[None, None, :], axis=1)
            xor_tab = jnp.bitwise_xor(irreps[:, None], irreps[None, :])
            pair_cnt = jnp.einsum("ak,bkl->abl", blk_cnt, blk_cnt[:, xor_tab])
            largest = jnp.max(pair_cnt[:, :, block_label])
            pair_cells = c_count * c_count
            caps = [t * pair_cells // 16 for t in TIERS]
            tier = sum((largest > cap).astype(jnp.int32) for cap in caps)
            own_irrep = blk_irrep[col_i]
            n_pb = pair_label.shape[0]
            pb = pair_rows // n_pb

            lab_jdc = jnp.bitwise_xor(blk_irrep[:, :, None], own_irrep[None, None, :])
            lab_bcd = jnp.bitwise_xor(own_irrep[None, :, None], blk_irrep[:, None, :])
            p_lab = pair_label.astype(lab_jdc.dtype)

            def compact(cap):
                def run(_):
                    int_jdc = jnp.transpose(integrals.reshape(c_count, n_col, c_count, ab_count), (1, 2, 0, 3))
                    int_jdc = int_jdc.reshape(cd_count, ab_count)
                    sent = compact_rows(
                        int_jdc, (lab_jdc == block_label[row_i])[None], pair_cells, cap, 1, ab_count
                    )
                    got = lax.all_gather(sent.T, "row", axis=0, tiled=False)
                    amp_jcd = jnp.transpose(amplitudes.reshape(pair_rows, c_count, n_col, c_count), (2, 1, 3, 0))
                    amp_jcd = amp_jcd.reshape(cd_count, pair_rows)
                    amp_dc = jnp.transpose(amplitudes.reshape(pair_rows, c_count, orb_width), (2, 1, 0))
                    amp_dc = amp_dc.reshape(cd_count, pair_rows)
                    outgoing = compact_rows(
                        amp_jcd, lab_bcd[None] == p_lab[:, None, None, None], pair_cells, cap, n_pb, pb
                    )
                    incoming = lax.all_to_all(outgoing, "col", split_axis=0, concat_axis=0, tiled=True)
                    direct = compact_rows(
                        amp_dc, lab_jdc[None] == p_lab[:, None, None, None], pair_cells, cap, n_pb, pb
                    )
                    both = jnp.concatenate([direct, incoming], axis=1)
                    match = (block_label[:, None] == pair_label[None, :]).astype(jnp.int32).reshape(n_row * n_pb)
                    diff = ladder_blocks(match, got, both, n_pb, pb)
                    return diff.reshape(n_row * ab_count, pair_rows)

                return run

            branches = [compact(cap) for cap in caps] + [dense]
            partial = lax.switch(tier, branches, None)
        parts = lax.all_to_all(
            partial.reshape(n_col, partial.shape[0] // n_col, pair_rows), "col", split_axis=0, concat_axis=0, tiled=True
        )
        return jnp.sum(parts, axis=0).astype(jnp.bfloat16)

    return body


def solution(mesh):
    placed = (P("row", "col"), P("col", "row"), P("row"), P(), P())
    return jax.shard_map(
        make_body(mesh.shape["row"], mesh.shape["col"]),
        mesh=mesh,
        in_specs=placed,
        out_specs=P("col", "row"),
        check_vma=False,
    )
```

```python
import jax
import jax.numpy as jnp
from jax import lax
from jax.experimental import pallas as pl
from jax.experimental.pallas import tpu as pltpu
from jax.sharding import PartitionSpec as P

PAIR_BLOCK = 128
IRREPS = 8
TIERS = (4, 5, 6, 8)


def _compact_kernel(base_ref, pos_ref, src_ref, out_ref, acc_ref, *, lists, width, sub, subs, steps):
    b = pl.program_id(0)
    span = sub + 16

    @pl.when(b == 0)
    def _():
        acc_ref[...] = jnp.zeros_like(acc_ref)

    rows = lax.broadcasted_iota(jnp.int32, (span, sub), 0)
    for l in range(lists):
        for k in range(subs):
            start = pl.multiple_of(base_ref[(l * steps + b) * subs + k], 16)
            onehot = (rows == pos_ref[l:l + 1, k * sub:(k + 1) * sub] - start).astype(src_ref.dtype)
            part = jnp.dot(
                onehot, src_ref[k * sub:(k + 1) * sub, l * width:(l + 1) * width], preferred_element_type=jnp.float32
            )
            acc_ref[pl.ds(start, span), l * width:(l + 1) * width] += part

    @pl.when(b == steps - 1)
    def _():
        out_ref[...] = acc_ref[: out_ref.shape[0], :].astype(out_ref.dtype)


def compact_rows(source, masks, chunk, cap, lists, width):
    total, _ = source.shape
    chunks = total // chunk
    sub = min(128, chunk)
    step = min(2048, chunk)
    steps = total // step
    flat = masks.reshape(lists, chunks, chunk).astype(jnp.int32)
    rank = jnp.cumsum(flat, axis=2) - flat
    offset = jnp.arange(chunks, dtype=jnp.int32)[None, :, None] * cap
    pos = jnp.where((flat > 0) & (rank < cap), offset + rank, -1).reshape(lists, total)
    first = (offset + jnp.minimum(rank, cap)).reshape(lists, total // sub, sub)[:, :, 0]
    base = ((first // 16) * 16).reshape(lists * (total // sub))
    kept = chunks * cap
    return pl.pallas_call(
        lambda *refs: _compact_kernel(*refs, lists=lists, width=width, sub=sub, subs=step // sub, steps=steps),
        out_shape=jax.ShapeDtypeStruct((kept, lists * width), source.dtype),
        grid_spec=pltpu.PrefetchScalarGridSpec(
            num_scalar_prefetch=1,
            grid=(steps,),
            in_specs=[
                pl.BlockSpec((lists, step), lambda b, base: (0, b)),
                pl.BlockSpec((step, lists * width), lambda b, base: (b, 0)),
            ],
            out_specs=pl.BlockSpec((kept, lists * width), lambda b, base: (0, 0)),
            scratch_shapes=[pltpu.VMEM((kept + sub + 16, lists * width), jnp.float32)],
        ),
        compiler_params=pltpu.CompilerParams(dimension_semantics=("arbitrary",)),
    )(base, pos, source)


def make_body(n_row, n_col):
    def body(amplitudes, integrals, pair_label, orbital_irrep, column_label):
        pair_rows, cd_count = amplitudes.shape
        orb_width = orbital_irrep.shape[0]
        c_count = cd_count // orb_width
        ab_count = integrals.shape[1]
        col_i = lax.axis_index("col")
        row_i = lax.axis_index("row")
        c_irrep = lax.dynamic_slice_in_dim(orbital_irrep, col_i * c_count, c_count)
        cd_label = jnp.bitwise_xor(c_irrep[:, None], orbital_irrep[None, :]).reshape(cd_count)
        row_label = jnp.repeat(pair_label, pair_rows // pair_label.shape[0])

        def dense(_):
            int_cube = integrals.reshape(c_count, orb_width, ab_count)
            swapped = lax.all_to_all(int_cube, "col", split_axis=1, concat_axis=0, tiled=True)
            mirrored = jnp.transpose(swapped, (1, 0, 2)).reshape(cd_count, ab_count)
            ab_label = jnp.repeat(column_label, PAIR_BLOCK)
            amp_keep = row_label[:, None] == cd_label[None, :]
            slab_keep = cd_label[:, None] == ab_label[None, :]
            amp_kept = jnp.where(amp_keep, amplitudes, jnp.zeros_like(amplitudes))
            int_slab = lax.all_gather(integrals, "row", axis=1, tiled=True)
            mirror_slab = lax.all_gather(mirrored, "row", axis=1, tiled=True)
            int_kept = jnp.where(slab_keep, int_slab, jnp.zeros_like(int_slab))
            mirror_kept = jnp.where(slab_keep, mirror_slab, jnp.zeros_like(mirror_slab))
            direct = jnp.einsum("ka,pk->ap", int_kept, amp_kept, preferred_element_type=jnp.float32)
            crossed = jnp.einsum("ka,pk->ap", mirror_kept, amp_kept, preferred_element_type=jnp.float32)
            return direct - crossed

        single = ab_count <= PAIR_BLOCK and PAIR_BLOCK % ab_count == 0
        if not single:
            partial = dense(None)
        else:
            block_label = column_label[(jnp.arange(n_row) * ab_count) // PAIR_BLOCK]
            irreps = jnp.arange(IRREPS, dtype=orbital_irrep.dtype)
            blk_irrep = orbital_irrep.reshape(n_col, c_count)
            blk_cnt = jnp.sum(blk_irrep[:, :, None] == irreps[None, None, :], axis=1)
            xor_tab = jnp.bitwise_xor(irreps[:, None], irreps[None, :])
            pair_cnt = jnp.einsum("ak,bkl->abl", blk_cnt, blk_cnt[:, xor_tab])
            largest = jnp.max(pair_cnt[:, :, block_label])
            pair_cells = c_count * c_count
            caps = [t * pair_cells // 16 for t in TIERS]
            tier = sum((largest > cap).astype(jnp.int32) for cap in caps)
            own_irrep = blk_irrep[col_i]
            n_pb = pair_label.shape[0]
            pb = pair_rows // n_pb

            lab_jdc = jnp.bitwise_xor(blk_irrep[:, :, None], own_irrep[None, None, :])
            lab_bcd = jnp.bitwise_xor(own_irrep[None, :, None], blk_irrep[:, None, :])
            p_lab = pair_label.astype(lab_jdc.dtype)

            def compact(cap):
                def run(_):
                    int_jdc = jnp.transpose(integrals.reshape(c_count, n_col, c_count, ab_count), (1, 2, 0, 3))
                    int_jdc = int_jdc.reshape(cd_count, ab_count)
                    sent = compact_rows(
                        int_jdc, (lab_jdc == block_label[row_i])[None], pair_cells, cap, 1, ab_count
                    )
                    got = lax.all_gather(sent, "row", axis=0, tiled=False)
                    amp_jcd = jnp.transpose(amplitudes.reshape(pair_rows, c_count, n_col, c_count), (2, 1, 3, 0))
                    amp_jcd = amp_jcd.reshape(cd_count, pair_rows)
                    amp_dc = jnp.transpose(amplitudes.reshape(pair_rows, c_count, orb_width), (2, 1, 0))
                    amp_dc = amp_dc.reshape(cd_count, pair_rows)
                    outgoing = compact_rows(
                        amp_jcd, lab_bcd[None] == p_lab[:, None, None, None], pair_cells, cap, n_pb, pb
                    )
                    incoming = lax.all_to_all(outgoing, "col", split_axis=0, concat_axis=0, tiled=True)
                    direct = compact_rows(
                        amp_dc, lab_jdc[None] == p_lab[:, None, None, None], pair_cells, cap, n_pb, pb
                    )
                    both = jnp.concatenate([direct, incoming], axis=1)
                    prod = jnp.einsum("imq,mx->iqx", got, both, preferred_element_type=jnp.float32)
                    diff = prod[..., :pair_rows] - prod[..., pair_rows:]
                    keep = block_label[:, None] == row_label[None, :]
                    diff = jnp.where(keep[:, None, :], diff, jnp.zeros_like(diff))
                    return diff.reshape(n_row * ab_count, pair_rows)

                return run

            branches = [compact(cap) for cap in caps] + [dense]
            partial = lax.switch(tier, branches, None)
        parts = lax.all_to_all(
            partial.reshape(n_col, partial.shape[0] // n_col, pair_rows), "col", split_axis=0, concat_axis=0, tiled=True
        )
        return jnp.sum(parts, axis=0).astype(jnp.bfloat16)

    return body


def solution(mesh):
    placed = (P("row", "col"), P("col", "row"), P("row"), P(), P())
    return jax.shard_map(
        make_body(mesh.shape["row"], mesh.shape["col"]),
        mesh=mesh,
        in_specs=placed,
        out_specs=P("col", "row"),
        check_vma=False,
    )
```

```python
import jax
import jax.numpy as jnp
from jax import lax
from jax.experimental import pallas as pl
from jax.experimental.pallas import tpu as pltpu
from jax.sharding import PartitionSpec as P

PAIR_BLOCK = 128
IRREPS = 8
TIERS = (4, 5, 6, 8)


def _compact_kernel(base_ref, pos_ref, src_ref, out_ref, acc_ref, *, lists, width, sub, subs, steps):
    b = pl.program_id(0)
    span = sub + 16

    @pl.when(b == 0)
    def _():
        acc_ref[...] = jnp.zeros_like(acc_ref)

    rows = lax.broadcasted_iota(jnp.int32, (span, sub), 0)
    for l in range(lists):
        for k in range(subs):
            start = pl.multiple_of(base_ref[(l * steps + b) * subs + k], 16)
            onehot = (rows == pos_ref[l:l + 1, k * sub:(k + 1) * sub] - start).astype(src_ref.dtype)
            part = jnp.dot(
                onehot, src_ref[k * sub:(k + 1) * sub, l * width:(l + 1) * width], preferred_element_type=jnp.float32
            )
            acc_ref[pl.ds(start, span), l * width:(l + 1) * width] += part

    @pl.when(b == steps - 1)
    def _():
        out_ref[...] = acc_ref[: out_ref.shape[0], :].astype(out_ref.dtype)


def compact_rows(source, masks, chunk, cap, lists, width):
    total, _ = source.shape
    chunks = total // chunk
    sub = min(128, chunk)
    step = min(2048, chunk)
    steps = total // step
    flat = masks.reshape(lists, chunks, chunk).astype(jnp.int32)
    rank = jnp.cumsum(flat, axis=2) - flat
    offset = jnp.arange(chunks, dtype=jnp.int32)[None, :, None] * cap
    pos = jnp.where((flat > 0) & (rank < cap), offset + rank, -1).reshape(lists, total)
    first = (offset + jnp.minimum(rank, cap)).reshape(lists, total // sub, sub)[:, :, 0]
    base = ((first // 16) * 16).reshape(lists * (total // sub))
    kept = chunks * cap
    return pl.pallas_call(
        lambda *refs: _compact_kernel(*refs, lists=lists, width=width, sub=sub, subs=step // sub, steps=steps),
        out_shape=jax.ShapeDtypeStruct((kept, lists * width), source.dtype),
        grid_spec=pltpu.PrefetchScalarGridSpec(
            num_scalar_prefetch=1,
            grid=(steps,),
            in_specs=[
                pl.BlockSpec((lists, step), lambda b, base: (0, b)),
                pl.BlockSpec((step, lists * width), lambda b, base: (b, 0)),
            ],
            out_specs=pl.BlockSpec((kept, lists * width), lambda b, base: (0, 0)),
            scratch_shapes=[pltpu.VMEM((kept + sub + 16, lists * width), jnp.float32)],
        ),
        compiler_params=pltpu.CompilerParams(dimension_semantics=("arbitrary",)),
    )(base, pos, source)


def physical_ring(devices):
    spots = [tuple(d.coords) for d in devices]
    n = len(spots)
    near = [[j for j in range(n) if sum(abs(a - b) for a, b in zip(spots[i], spots[j])) == 1] for i in range(n)]
    path = [0]
    used = {0}

    def grow():
        if len(path) == n:
            return 0 in near[path[-1]]
        for j in near[path[-1]]:
            if j not in used:
                path.append(j)
                used.add(j)
                if grow():
                    return True
                path.pop()
                used.discard(j)
        return False

    return path if n > 2 and grow() else None


def ring_gather(block, ring, n):
    order = jnp.asarray(ring, jnp.int32)
    place = jnp.asarray([ring.index(r) for r in range(n)], jnp.int32)
    here = place[lax.axis_index("row")]
    ahead = [(ring[k], ring[(k + 1) % n]) for k in range(n)]
    behind = [(b, a) for a, b in ahead]
    got = jnp.zeros((n,) + block.shape, block.dtype)
    got = lax.dynamic_update_index_in_dim(got, block, order[here], 0)
    fwd = bwd = block
    half = block.shape[0] // 2
    for s in range(1, n // 2 + 1):
        if s < n // 2 or n % 2:
            fwd = lax.ppermute(fwd, "row", ahead)
            bwd = lax.ppermute(bwd, "row", behind)
            got = lax.dynamic_update_index_in_dim(got, fwd, order[(here - s) % n], 0)
            got = lax.dynamic_update_index_in_dim(got, bwd, order[(here + s) % n], 0)
        else:
            top = lax.ppermute(fwd[:half], "row", ahead)
            low = lax.ppermute(bwd[half:], "row", behind)
            got = lax.dynamic_update_index_in_dim(got, jnp.concatenate([top, low]), order[(here - s) % n], 0)
    return got


def make_body(n_row, n_col, ring=None):
    def body(amplitudes, integrals, pair_label, orbital_irrep, column_label):
        pair_rows, cd_count = amplitudes.shape
        orb_width = orbital_irrep.shape[0]
        c_count = cd_count // orb_width
        ab_count = integrals.shape[1]
        col_i = lax.axis_index("col")
        row_i = lax.axis_index("row")
        c_irrep = lax.dynamic_slice_in_dim(orbital_irrep, col_i * c_count, c_count)
        cd_label = jnp.bitwise_xor(c_irrep[:, None], orbital_irrep[None, :]).reshape(cd_count)
        row_label = jnp.repeat(pair_label, pair_rows // pair_label.shape[0])

        def dense(_):
            int_cube = integrals.reshape(c_count, orb_width, ab_count)
            swapped = lax.all_to_all(int_cube, "col", split_axis=1, concat_axis=0, tiled=True)
            mirrored = jnp.transpose(swapped, (1, 0, 2)).reshape(cd_count, ab_count)
            ab_label = jnp.repeat(column_label, PAIR_BLOCK)
            amp_keep = row_label[:, None] == cd_label[None, :]
            slab_keep = cd_label[:, None] == ab_label[None, :]
            amp_kept = jnp.where(amp_keep, amplitudes, jnp.zeros_like(amplitudes))
            int_slab = lax.all_gather(integrals, "row", axis=1, tiled=True)
            mirror_slab = lax.all_gather(mirrored, "row", axis=1, tiled=True)
            int_kept = jnp.where(slab_keep, int_slab, jnp.zeros_like(int_slab))
            mirror_kept = jnp.where(slab_keep, mirror_slab, jnp.zeros_like(mirror_slab))
            direct = jnp.einsum("ka,pk->ap", int_kept, amp_kept, preferred_element_type=jnp.float32)
            crossed = jnp.einsum("ka,pk->ap", mirror_kept, amp_kept, preferred_element_type=jnp.float32)
            return direct - crossed

        single = ab_count <= PAIR_BLOCK and PAIR_BLOCK % ab_count == 0
        if not single:
            partial = dense(None)
        else:
            block_label = column_label[(jnp.arange(n_row) * ab_count) // PAIR_BLOCK]
            irreps = jnp.arange(IRREPS, dtype=orbital_irrep.dtype)
            blk_irrep = orbital_irrep.reshape(n_col, c_count)
            blk_cnt = jnp.sum(blk_irrep[:, :, None] == irreps[None, None, :], axis=1)
            xor_tab = jnp.bitwise_xor(irreps[:, None], irreps[None, :])
            pair_cnt = jnp.einsum("ak,bkl->abl", blk_cnt, blk_cnt[:, xor_tab])
            largest = jnp.max(pair_cnt[:, :, block_label])
            pair_cells = c_count * c_count
            caps = [t * pair_cells // 16 for t in TIERS]
            tier = sum((largest > cap).astype(jnp.int32) for cap in caps)
            own_irrep = blk_irrep[col_i]
            n_pb = pair_label.shape[0]
            pb = pair_rows // n_pb

            lab_jdc = jnp.bitwise_xor(blk_irrep[:, :, None], own_irrep[None, None, :])
            lab_bcd = jnp.bitwise_xor(own_irrep[None, :, None], blk_irrep[:, None, :])
            p_lab = pair_label.astype(lab_jdc.dtype)

            def compact(cap):
                def run(_):
                    int_jdc = jnp.transpose(integrals.reshape(c_count, n_col, c_count, ab_count), (1, 2, 0, 3))
                    int_jdc = int_jdc.reshape(cd_count, ab_count)
                    sent = compact_rows(
                        int_jdc, (lab_jdc == block_label[row_i])[None], pair_cells, cap, 1, ab_count
                    )
                    if ring is None:
                        got = lax.all_gather(sent, "row", axis=0, tiled=False)
                    else:
                        got = ring_gather(sent, ring, n_row)
                    amp_jcd = jnp.transpose(amplitudes.reshape(pair_rows, c_count, n_col, c_count), (2, 1, 3, 0))
                    amp_jcd = amp_jcd.reshape(cd_count, pair_rows)
                    amp_dc = jnp.transpose(amplitudes.reshape(pair_rows, c_count, orb_width), (2, 1, 0))
                    amp_dc = amp_dc.reshape(cd_count, pair_rows)
                    outgoing = compact_rows(
                        amp_jcd, lab_bcd[None] == p_lab[:, None, None, None], pair_cells, cap, n_pb, pb
                    )
                    incoming = lax.all_to_all(outgoing, "col", split_axis=0, concat_axis=0, tiled=True)
                    direct = compact_rows(
                        amp_dc, lab_jdc[None] == p_lab[:, None, None, None], pair_cells, cap, n_pb, pb
                    )
                    both = jnp.concatenate([direct, incoming], axis=1)
                    prod = jnp.einsum("imq,mx->iqx", got, both, preferred_element_type=jnp.float32)
                    diff = prod[..., :pair_rows] - prod[..., pair_rows:]
                    keep = block_label[:, None] == row_label[None, :]
                    diff = jnp.where(keep[:, None, :], diff, jnp.zeros_like(diff))
                    return diff.reshape(n_row * ab_count, pair_rows)

                return run

            branches = [compact(cap) for cap in caps] + [dense]
            partial = lax.switch(tier, branches, None)
        parts = lax.all_to_all(
            partial.reshape(n_col, partial.shape[0] // n_col, pair_rows), "col", split_axis=0, concat_axis=0, tiled=True
        )
        return jnp.sum(parts, axis=0).astype(jnp.bfloat16)

    return body


def solution(mesh):
    axes = list(mesh.axis_names)
    row_devices = mesh.devices.transpose([axes.index("row"), axes.index("col")])[:, 0]
    try:
        ring = physical_ring(list(row_devices))
    except AttributeError:
        ring = None
    placed = (P("row", "col"), P("col", "row"), P("row"), P(), P())
    return jax.shard_map(
        make_body(mesh.shape["row"], mesh.shape["col"], ring),
        mesh=mesh,
        in_specs=placed,
        out_specs=P("col", "row"),
        check_vma=False,
    )
```

```python
import jax
import jax.numpy as jnp
from jax import lax
from jax.experimental import pallas as pl
from jax.experimental.pallas import tpu as pltpu
from jax.sharding import PartitionSpec as P

PAIR_BLOCK = 128
IRREPS = 8
TIERS = (8, 9, 10, 12, 16)


def _compact_kernel(base_ref, pos_ref, src_ref, out_ref, acc_ref, *, lists, width, sub, subs, steps):
    b = pl.program_id(0)
    span = sub + 16

    @pl.when(b == 0)
    def _():
        acc_ref[...] = jnp.zeros_like(acc_ref)

    rows = lax.broadcasted_iota(jnp.int32, (span, sub), 0)
    for l in range(lists):
        for k in range(subs):
            start = pl.multiple_of(base_ref[(l * steps + b) * subs + k], 16)
            onehot = (rows == pos_ref[l:l + 1, k * sub:(k + 1) * sub] - start).astype(src_ref.dtype)
            part = jnp.dot(
                onehot, src_ref[k * sub:(k + 1) * sub, l * width:(l + 1) * width], preferred_element_type=jnp.float32
            )
            acc_ref[pl.ds(start, span), l * width:(l + 1) * width] += part

    @pl.when(b == steps - 1)
    def _():
        out_ref[...] = acc_ref[: out_ref.shape[0], :].astype(out_ref.dtype)


def compact_rows(source, masks, chunk, cap, lists, width):
    total, _ = source.shape
    chunks = total // chunk
    sub = min(128, chunk)
    step = min(2048, chunk)
    steps = total // step
    flat = masks.reshape(lists, chunks, chunk).astype(jnp.int32)
    rank = jnp.cumsum(flat, axis=2) - flat
    offset = jnp.arange(chunks, dtype=jnp.int32)[None, :, None] * cap
    pos = jnp.where((flat > 0) & (rank < cap), offset + rank, -1).reshape(lists, total)
    first = (offset + jnp.minimum(rank, cap)).reshape(lists, total // sub, sub)[:, :, 0]
    base = ((first // 16) * 16).reshape(lists * (total // sub))
    kept = chunks * cap
    return pl.pallas_call(
        lambda *refs: _compact_kernel(*refs, lists=lists, width=width, sub=sub, subs=step // sub, steps=steps),
        out_shape=jax.ShapeDtypeStruct((kept, lists * width), source.dtype),
        grid_spec=pltpu.PrefetchScalarGridSpec(
            num_scalar_prefetch=1,
            grid=(steps,),
            in_specs=[
                pl.BlockSpec((lists, step), lambda b, base: (0, b)),
                pl.BlockSpec((step, lists * width), lambda b, base: (b, 0)),
            ],
            out_specs=pl.BlockSpec((kept, lists * width), lambda b, base: (0, 0)),
            scratch_shapes=[pltpu.VMEM((kept + sub + 16, lists * width), jnp.float32)],
        ),
        compiler_params=pltpu.CompilerParams(dimension_semantics=("arbitrary",)),
    )(base, pos, source)


def make_body(n_row, n_col):
    def body(amplitudes, integrals, pair_label, orbital_irrep, column_label):
        pair_rows, cd_count = amplitudes.shape
        orb_width = orbital_irrep.shape[0]
        c_count = cd_count // orb_width
        ab_count = integrals.shape[1]
        col_i = lax.axis_index("col")
        row_i = lax.axis_index("row")
        c_irrep = lax.dynamic_slice_in_dim(orbital_irrep, col_i * c_count, c_count)
        cd_label = jnp.bitwise_xor(c_irrep[:, None], orbital_irrep[None, :]).reshape(cd_count)
        row_label = jnp.repeat(pair_label, pair_rows // pair_label.shape[0])

        def dense(_):
            int_cube = integrals.reshape(c_count, orb_width, ab_count)
            swapped = lax.all_to_all(int_cube, "col", split_axis=1, concat_axis=0, tiled=True)
            mirrored = jnp.transpose(swapped, (1, 0, 2)).reshape(cd_count, ab_count)
            ab_label = jnp.repeat(column_label, PAIR_BLOCK)
            amp_keep = row_label[:, None] == cd_label[None, :]
            slab_keep = cd_label[:, None] == ab_label[None, :]
            amp_kept = jnp.where(amp_keep, amplitudes, jnp.zeros_like(amplitudes))
            int_slab = lax.all_gather(integrals, "row", axis=1, tiled=True)
            mirror_slab = lax.all_gather(mirrored, "row", axis=1, tiled=True)
            int_kept = jnp.where(slab_keep, int_slab, jnp.zeros_like(int_slab))
            mirror_kept = jnp.where(slab_keep, mirror_slab, jnp.zeros_like(mirror_slab))
            direct = jnp.einsum("ka,pk->ap", int_kept, amp_kept, preferred_element_type=jnp.float32)
            crossed = jnp.einsum("ka,pk->ap", mirror_kept, amp_kept, preferred_element_type=jnp.float32)
            return direct - crossed

        single = ab_count <= PAIR_BLOCK and PAIR_BLOCK % ab_count == 0
        if not single:
            partial = dense(None)
        else:
            block_label = column_label[(jnp.arange(n_row) * ab_count) // PAIR_BLOCK]
            irreps = jnp.arange(IRREPS, dtype=orbital_irrep.dtype)
            blk_irrep = orbital_irrep.reshape(n_col, c_count)
            blk_cnt = jnp.sum(blk_irrep[:, :, None] == irreps[None, None, :], axis=1)
            xor_tab = jnp.bitwise_xor(irreps[:, None], irreps[None, :])
            pair_cnt = jnp.einsum("ak,bkl->abl", blk_cnt, blk_cnt[:, xor_tab])
            largest = jnp.max(pair_cnt[:, :, block_label])
            pair_cells = c_count * c_count
            caps = [t * pair_cells // 32 for t in TIERS]
            tier = sum((largest > cap).astype(jnp.int32) for cap in caps)
            own_irrep = blk_irrep[col_i]
            n_pb = pair_label.shape[0]
            pb = pair_rows // n_pb

            lab_jdc = jnp.bitwise_xor(blk_irrep[:, :, None], own_irrep[None, None, :])
            lab_bcd = jnp.bitwise_xor(own_irrep[None, :, None], blk_irrep[:, None, :])
            p_lab = pair_label.astype(lab_jdc.dtype)

            def compact(cap):
                def run(_):
                    int_jdc = jnp.transpose(integrals.reshape(c_count, n_col, c_count, ab_count), (1, 2, 0, 3))
                    int_jdc = int_jdc.reshape(cd_count, ab_count)
                    sent = compact_rows(
                        int_jdc, (lab_jdc == block_label[row_i])[None], pair_cells, cap, 1, ab_count
                    )
                    got = lax.all_gather(sent, "row", axis=0, tiled=False)
                    amp_jcd = jnp.transpose(amplitudes.reshape(pair_rows, c_count, n_col, c_count), (2, 1, 3, 0))
                    amp_jcd = amp_jcd.reshape(cd_count, pair_rows)
                    amp_dc = jnp.transpose(amplitudes.reshape(pair_rows, c_count, orb_width), (2, 1, 0))
                    amp_dc = amp_dc.reshape(cd_count, pair_rows)
                    outgoing = compact_rows(
                        amp_jcd, lab_bcd[None] == p_lab[:, None, None, None], pair_cells, cap, n_pb, pb
                    )
                    incoming = lax.all_to_all(outgoing, "col", split_axis=0, concat_axis=0, tiled=True)
                    direct = compact_rows(
                        amp_dc, lab_jdc[None] == p_lab[:, None, None, None], pair_cells, cap, n_pb, pb
                    )
                    both = jnp.concatenate([direct, incoming], axis=1)
                    prod = jnp.einsum("imq,mx->iqx", got, both, preferred_element_type=jnp.float32)
                    diff = prod[..., :pair_rows] - prod[..., pair_rows:]
                    keep = block_label[:, None] == row_label[None, :]
                    diff = jnp.where(keep[:, None, :], diff, jnp.zeros_like(diff))
                    return diff.reshape(n_row * ab_count, pair_rows)

                return run

            branches = [compact(cap) for cap in caps] + [dense]
            partial = lax.switch(tier, branches, None)
        parts = lax.all_to_all(
            partial.reshape(n_col, partial.shape[0] // n_col, pair_rows), "col", split_axis=0, concat_axis=0, tiled=True
        )
        return jnp.sum(parts, axis=0).astype(jnp.bfloat16)

    return body


def solution(mesh):
    placed = (P("row", "col"), P("col", "row"), P("row"), P(), P())
    return jax.shard_map(
        make_body(mesh.shape["row"], mesh.shape["col"]),
        mesh=mesh,
        in_specs=placed,
        out_specs=P("col", "row"),
        check_vma=False,
    )
```

```python
import jax
import jax.numpy as jnp
from jax import lax
from jax.experimental import pallas as pl
from jax.experimental.pallas import tpu as pltpu
from jax.sharding import PartitionSpec as P

PAIR_BLOCK = 128
IRREPS = 8
TIERS = (8, 9, 10, 12, 16)


def _compact_kernel(base_ref, pos_ref, src_ref, out_ref, acc_ref, *, lists, width, sub, subs, steps):
    b = pl.program_id(0)
    span = sub + 16

    @pl.when(b == 0)
    def _():
        acc_ref[...] = jnp.zeros_like(acc_ref)

    rows = lax.broadcasted_iota(jnp.int32, (span, sub), 0)
    for l in range(lists):
        for k in range(subs):
            start = pl.multiple_of(base_ref[(l * steps + b) * subs + k], 16)
            onehot = (rows == pos_ref[l:l + 1, k * sub:(k + 1) * sub] - start).astype(src_ref.dtype)
            part = jnp.dot(
                onehot, src_ref[k * sub:(k + 1) * sub, l * width:(l + 1) * width], preferred_element_type=jnp.float32
            )
            acc_ref[pl.ds(start, span), l * width:(l + 1) * width] += part

    @pl.when(b == steps - 1)
    def _():
        out_ref[...] = acc_ref[: out_ref.shape[0], :].astype(out_ref.dtype)


def compact_rows(source, masks, chunk, cap, lists, width):
    total, _ = source.shape
    chunks = total // chunk
    sub = min(128, chunk)
    step = min(4096 if lists == 1 else 2048, chunk)
    steps = total // step
    flat = masks.reshape(lists, chunks, chunk).astype(jnp.int32)
    rank = jnp.cumsum(flat, axis=2) - flat
    offset = jnp.arange(chunks, dtype=jnp.int32)[None, :, None] * cap
    pos = jnp.where((flat > 0) & (rank < cap), offset + rank, -1).reshape(lists, total)
    first = (offset + jnp.minimum(rank, cap)).reshape(lists, total // sub, sub)[:, :, 0]
    base = ((first // 16) * 16).reshape(lists * (total // sub))
    kept = chunks * cap
    return pl.pallas_call(
        lambda *refs: _compact_kernel(*refs, lists=lists, width=width, sub=sub, subs=step // sub, steps=steps),
        out_shape=jax.ShapeDtypeStruct((kept, lists * width), source.dtype),
        grid_spec=pltpu.PrefetchScalarGridSpec(
            num_scalar_prefetch=1,
            grid=(steps,),
            in_specs=[
                pl.BlockSpec((lists, step), lambda b, base: (0, b)),
                pl.BlockSpec((step, lists * width), lambda b, base: (b, 0)),
            ],
            out_specs=pl.BlockSpec((kept, lists * width), lambda b, base: (0, 0)),
            scratch_shapes=[pltpu.VMEM((kept + sub + 16, lists * width), jnp.float32)],
        ),
        compiler_params=pltpu.CompilerParams(dimension_semantics=("arbitrary",)),
    )(base, pos, source)


def make_body(n_row, n_col):
    def body(amplitudes, integrals, pair_label, orbital_irrep, column_label):
        pair_rows, cd_count = amplitudes.shape
        orb_width = orbital_irrep.shape[0]
        c_count = cd_count // orb_width
        ab_count = integrals.shape[1]
        col_i = lax.axis_index("col")
        row_i = lax.axis_index("row")
        c_irrep = lax.dynamic_slice_in_dim(orbital_irrep, col_i * c_count, c_count)
        cd_label = jnp.bitwise_xor(c_irrep[:, None], orbital_irrep[None, :]).reshape(cd_count)
        row_label = jnp.repeat(pair_label, pair_rows // pair_label.shape[0])

        def dense(_):
            int_cube = integrals.reshape(c_count, orb_width, ab_count)
            swapped = lax.all_to_all(int_cube, "col", split_axis=1, concat_axis=0, tiled=True)
            mirrored = jnp.transpose(swapped, (1, 0, 2)).reshape(cd_count, ab_count)
            ab_label = jnp.repeat(column_label, PAIR_BLOCK)
            amp_keep = row_label[:, None] == cd_label[None, :]
            slab_keep = cd_label[:, None] == ab_label[None, :]
            amp_kept = jnp.where(amp_keep, amplitudes, jnp.zeros_like(amplitudes))
            int_slab = lax.all_gather(integrals, "row", axis=1, tiled=True)
            mirror_slab = lax.all_gather(mirrored, "row", axis=1, tiled=True)
            int_kept = jnp.where(slab_keep, int_slab, jnp.zeros_like(int_slab))
            mirror_kept = jnp.where(slab_keep, mirror_slab, jnp.zeros_like(mirror_slab))
            direct = jnp.einsum("ka,pk->ap", int_kept, amp_kept, preferred_element_type=jnp.float32)
            crossed = jnp.einsum("ka,pk->ap", mirror_kept, amp_kept, preferred_element_type=jnp.float32)
            return direct - crossed

        single = ab_count <= PAIR_BLOCK and PAIR_BLOCK % ab_count == 0
        if not single:
            partial = dense(None)
        else:
            block_label = column_label[(jnp.arange(n_row) * ab_count) // PAIR_BLOCK]
            irreps = jnp.arange(IRREPS, dtype=orbital_irrep.dtype)
            blk_irrep = orbital_irrep.reshape(n_col, c_count)
            blk_cnt = jnp.sum(blk_irrep[:, :, None] == irreps[None, None, :], axis=1)
            xor_tab = jnp.bitwise_xor(irreps[:, None], irreps[None, :])
            pair_cnt = jnp.einsum("ak,bkl->abl", blk_cnt, blk_cnt[:, xor_tab])
            largest = jnp.max(pair_cnt[:, :, block_label])
            pair_cells = c_count * c_count
            caps = [t * pair_cells // 32 for t in TIERS]
            tier = sum((largest > cap).astype(jnp.int32) for cap in caps)
            own_irrep = blk_irrep[col_i]
            n_pb = pair_label.shape[0]
            pb = pair_rows // n_pb

            lab_jdc = jnp.bitwise_xor(blk_irrep[:, :, None], own_irrep[None, None, :])
            lab_bcd = jnp.bitwise_xor(own_irrep[None, :, None], blk_irrep[:, None, :])
            p_lab = pair_label.astype(lab_jdc.dtype)

            def compact(cap):
                def run(_):
                    int_jdc = jnp.transpose(integrals.reshape(c_count, n_col, c_count, ab_count), (1, 2, 0, 3))
                    int_jdc = int_jdc.reshape(cd_count, ab_count)
                    sent = compact_rows(
                        int_jdc, (lab_jdc == block_label[row_i])[None], pair_cells, cap, 1, ab_count
                    )
                    got = lax.all_gather(sent, "row", axis=0, tiled=False)
                    amp_jcd = jnp.transpose(amplitudes.reshape(pair_rows, c_count, n_col, c_count), (2, 1, 3, 0))
                    amp_jcd = amp_jcd.reshape(cd_count, pair_rows)
                    amp_dc = jnp.transpose(amplitudes.reshape(pair_rows, c_count, orb_width), (2, 1, 0))
                    amp_dc = amp_dc.reshape(cd_count, pair_rows)
                    outgoing = compact_rows(
                        amp_jcd, lab_bcd[None] == p_lab[:, None, None, None], pair_cells, cap, n_pb, pb
                    )
                    incoming = lax.all_to_all(outgoing, "col", split_axis=0, concat_axis=0, tiled=True)
                    direct = compact_rows(
                        amp_dc, lab_jdc[None] == p_lab[:, None, None, None], pair_cells, cap, n_pb, pb
                    )
                    both = jnp.concatenate([direct, incoming], axis=1)
                    prod = jnp.einsum("imq,mx->iqx", got, both, preferred_element_type=jnp.float32)
                    diff = prod[..., :pair_rows] - prod[..., pair_rows:]
                    keep = block_label[:, None] == row_label[None, :]
                    diff = jnp.where(keep[:, None, :], diff, jnp.zeros_like(diff))
                    return diff.reshape(n_row * ab_count, pair_rows)

                return run

            branches = [compact(cap) for cap in caps] + [dense]
            partial = lax.switch(tier, branches, None)
        parts = lax.all_to_all(
            partial.reshape(n_col, partial.shape[0] // n_col, pair_rows), "col", split_axis=0, concat_axis=0, tiled=True
        )
        return jnp.sum(parts, axis=0).astype(jnp.bfloat16)

    return body


def solution(mesh):
    placed = (P("row", "col"), P("col", "row"), P("row"), P(), P())
    return jax.shard_map(
        make_body(mesh.shape["row"], mesh.shape["col"]),
        mesh=mesh,
        in_specs=placed,
        out_specs=P("col", "row"),
        check_vma=False,
    )
```

```python
import jax
import jax.numpy as jnp
from jax import lax
from jax.experimental import pallas as pl
from jax.experimental.pallas import tpu as pltpu
from jax.sharding import PartitionSpec as P

PAIR_BLOCK = 128
IRREPS = 8
TIERS = (8, 9, 10, 12, 16)


def _compact_kernel(base_ref, pos_ref, src_ref, out_ref, acc_ref, *, lists, width, sub, subs, steps):
    b = pl.program_id(0)
    span = sub + 16

    @pl.when(b == 0)
    def _():
        acc_ref[...] = jnp.zeros_like(acc_ref)

    rows = lax.broadcasted_iota(jnp.int32, (span, sub), 0)
    for l in range(lists):
        for k in range(subs):
            start = pl.multiple_of(base_ref[(l * steps + b) * subs + k], 16)
            onehot = (rows == pos_ref[l:l + 1, k * sub:(k + 1) * sub] - start).astype(src_ref.dtype)
            part = jnp.dot(
                onehot, src_ref[k * sub:(k + 1) * sub, l * width:(l + 1) * width], preferred_element_type=jnp.float32
            )
            acc_ref[pl.ds(start, span), l * width:(l + 1) * width] += part

    @pl.when(b == steps - 1)
    def _():
        out_ref[...] = acc_ref[: out_ref.shape[0], :].astype(out_ref.dtype)


def compact_rows(source, masks, chunk, cap, lists, width):
    total, _ = source.shape
    chunks = total // chunk
    sub = min(128, chunk)
    step = min(4096 if lists == 1 else 2048, chunk)
    steps = total // step
    flat = masks.reshape(lists, chunks, chunk).astype(jnp.int32)
    rank = jnp.cumsum(flat, axis=2) - flat
    offset = jnp.arange(chunks, dtype=jnp.int32)[None, :, None] * cap
    pos = jnp.where((flat > 0) & (rank < cap), offset + rank, -1).reshape(lists, total)
    first = (offset + jnp.minimum(rank, cap)).reshape(lists, total // sub, sub)[:, :, 0]
    base = ((first // 16) * 16).reshape(lists * (total // sub))
    kept = chunks * cap
    return pl.pallas_call(
        lambda *refs: _compact_kernel(*refs, lists=lists, width=width, sub=sub, subs=step // sub, steps=steps),
        out_shape=jax.ShapeDtypeStruct((kept, lists * width), source.dtype),
        grid_spec=pltpu.PrefetchScalarGridSpec(
            num_scalar_prefetch=1,
            grid=(steps,),
            in_specs=[
                pl.BlockSpec((lists, step), lambda b, base: (0, b)),
                pl.BlockSpec((step, lists * width), lambda b, base: (b, 0)),
            ],
            out_specs=pl.BlockSpec((kept, lists * width), lambda b, base: (0, 0)),
            scratch_shapes=[pltpu.VMEM((kept + sub + 16, lists * width), jnp.float32)],
        ),
        compiler_params=pltpu.CompilerParams(dimension_semantics=("arbitrary",)),
    )(base, pos, source)


def make_body(n_row, n_col):
    def body(amplitudes, integrals, pair_label, orbital_irrep, column_label):
        pair_rows, cd_count = amplitudes.shape
        orb_width = orbital_irrep.shape[0]
        c_count = cd_count // orb_width
        ab_count = integrals.shape[1]
        col_i = lax.axis_index("col")
        row_i = lax.axis_index("row")
        c_irrep = lax.dynamic_slice_in_dim(orbital_irrep, col_i * c_count, c_count)
        cd_label = jnp.bitwise_xor(c_irrep[:, None], orbital_irrep[None, :]).reshape(cd_count)
        row_label = jnp.repeat(pair_label, pair_rows // pair_label.shape[0])

        def dense(_):
            int_cube = integrals.reshape(c_count, orb_width, ab_count)
            swapped = lax.all_to_all(int_cube, "col", split_axis=1, concat_axis=0, tiled=True)
            mirrored = jnp.transpose(swapped, (1, 0, 2)).reshape(cd_count, ab_count)
            ab_label = jnp.repeat(column_label, PAIR_BLOCK)
            amp_keep = row_label[:, None] == cd_label[None, :]
            slab_keep = cd_label[:, None] == ab_label[None, :]
            amp_kept = jnp.where(amp_keep, amplitudes, jnp.zeros_like(amplitudes))
            int_slab = lax.all_gather(integrals, "row", axis=1, tiled=True)
            mirror_slab = lax.all_gather(mirrored, "row", axis=1, tiled=True)
            int_kept = jnp.where(slab_keep, int_slab, jnp.zeros_like(int_slab))
            mirror_kept = jnp.where(slab_keep, mirror_slab, jnp.zeros_like(mirror_slab))
            direct = jnp.einsum("ka,pk->ap", int_kept, amp_kept, preferred_element_type=jnp.float32)
            crossed = jnp.einsum("ka,pk->ap", mirror_kept, amp_kept, preferred_element_type=jnp.float32)
            return direct - crossed

        single = ab_count <= PAIR_BLOCK and PAIR_BLOCK % ab_count == 0
        if not single:
            partial = dense(None)
        else:
            block_label = column_label[(jnp.arange(n_row) * ab_count) // PAIR_BLOCK]
            irreps = jnp.arange(IRREPS, dtype=orbital_irrep.dtype)
            blk_irrep = orbital_irrep.reshape(n_col, c_count)
            blk_cnt = jnp.sum(blk_irrep[:, :, None] == irreps[None, None, :], axis=1)
            xor_tab = jnp.bitwise_xor(irreps[:, None], irreps[None, :])
            pair_cnt = jnp.einsum("ak,bkl->abl", blk_cnt, blk_cnt[:, xor_tab])
            largest = jnp.max(pair_cnt[:, :, block_label])
            pair_cells = c_count * c_count
            caps = [t * pair_cells // 32 for t in TIERS]
            tier = sum((largest > cap).astype(jnp.int32) for cap in caps)
            own_irrep = blk_irrep[col_i]
            n_pb = pair_label.shape[0]
            pb = pair_rows // n_pb

            lab_jdc = jnp.bitwise_xor(blk_irrep[:, :, None], own_irrep[None, None, :])
            lab_bcd = jnp.bitwise_xor(own_irrep[None, :, None], blk_irrep[:, None, :])
            p_lab = pair_label.astype(lab_jdc.dtype)

            def compact(cap):
                def run(_):
                    int_jdc = jnp.transpose(integrals.reshape(c_count, n_col, c_count, ab_count), (1, 2, 0, 3))
                    int_jdc = int_jdc.reshape(cd_count, ab_count)
                    sent = compact_rows(
                        int_jdc, (lab_jdc == block_label[row_i])[None], pair_cells, cap, 1, ab_count
                    )
                    got = lax.all_gather(sent.T, "row", axis=0, tiled=False)
                    amp_jcd = jnp.transpose(amplitudes.reshape(pair_rows, c_count, n_col, c_count), (2, 1, 3, 0))
                    amp_jcd = amp_jcd.reshape(cd_count, pair_rows)
                    amp_dc = jnp.transpose(amplitudes.reshape(pair_rows, c_count, orb_width), (2, 1, 0))
                    amp_dc = amp_dc.reshape(cd_count, pair_rows)
                    outgoing = compact_rows(
                        amp_jcd, lab_bcd[None] == p_lab[:, None, None, None], pair_cells, cap, n_pb, pb
                    )
                    incoming = lax.all_to_all(outgoing, "col", split_axis=0, concat_axis=0, tiled=True)
                    direct = compact_rows(
                        amp_dc, lab_jdc[None] == p_lab[:, None, None, None], pair_cells, cap, n_pb, pb
                    )
                    both = jnp.concatenate([direct, incoming], axis=1)
                    prod = jnp.einsum("iqm,mx->iqx", got, both, preferred_element_type=jnp.float32)
                    diff = prod[..., :pair_rows] - prod[..., pair_rows:]
                    keep = block_label[:, None] == row_label[None, :]
                    diff = jnp.where(keep[:, None, :], diff, jnp.zeros_like(diff))
                    return diff.reshape(n_row * ab_count, pair_rows)

                return run

            branches = [compact(cap) for cap in caps] + [dense]
            partial = lax.switch(tier, branches, None)
        parts = lax.all_to_all(
            partial.reshape(n_col, partial.shape[0] // n_col, pair_rows), "col", split_axis=0, concat_axis=0, tiled=True
        )
        return jnp.sum(parts, axis=0).astype(jnp.bfloat16)

    return body


def solution(mesh):
    placed = (P("row", "col"), P("col", "row"), P("row"), P(), P())
    return jax.shard_map(
        make_body(mesh.shape["row"], mesh.shape["col"]),
        mesh=mesh,
        in_specs=placed,
        out_specs=P("col", "row"),
        check_vma=False,
    )
```

```python
import jax
import jax.numpy as jnp
from jax import lax
from jax.experimental import pallas as pl
from jax.experimental.pallas import tpu as pltpu
from jax.sharding import PartitionSpec as P

PAIR_BLOCK = 128
IRREPS = 8
TIERS = (8, 9, 10, 12, 16)


def _compact_kernel(base_ref, pos_ref, src_ref, out_ref, acc_ref, *, lists, width, sub, subs, steps):
    b = pl.program_id(0)
    span = sub + 16

    @pl.when(b == 0)
    def _():
        acc_ref[...] = jnp.zeros_like(acc_ref)

    rows = lax.broadcasted_iota(jnp.int32, (span, sub), 0)
    for l in range(lists):
        for k in range(subs):
            start = pl.multiple_of(base_ref[(l * steps + b) * subs + k], 16)
            onehot = (rows == pos_ref[l:l + 1, k * sub:(k + 1) * sub] - start).astype(src_ref.dtype)
            part = jnp.dot(
                onehot, src_ref[k * sub:(k + 1) * sub, l * width:(l + 1) * width], preferred_element_type=jnp.float32
            )
            acc_ref[pl.ds(start, span), l * width:(l + 1) * width] += part

    @pl.when(b == steps - 1)
    def _():
        out_ref[...] = acc_ref[: out_ref.shape[0], :].astype(out_ref.dtype)


def compact_rows(source, masks, chunk, cap, lists, width):
    total, _ = source.shape
    chunks = total // chunk
    sub = min(128, chunk)
    step = min(8192, total) if lists == 1 else min(2048, chunk)
    steps = total // step
    flat = masks.reshape(lists, chunks, chunk).astype(jnp.int32)
    rank = jnp.cumsum(flat, axis=2) - flat
    offset = jnp.arange(chunks, dtype=jnp.int32)[None, :, None] * cap
    pos = jnp.where((flat > 0) & (rank < cap), offset + rank, -1).reshape(lists, total)
    first = (offset + jnp.minimum(rank, cap)).reshape(lists, total // sub, sub)[:, :, 0]
    base = ((first // 16) * 16).reshape(lists * (total // sub))
    kept = chunks * cap
    return pl.pallas_call(
        lambda *refs: _compact_kernel(*refs, lists=lists, width=width, sub=sub, subs=step // sub, steps=steps),
        out_shape=jax.ShapeDtypeStruct((kept, lists * width), source.dtype),
        grid_spec=pltpu.PrefetchScalarGridSpec(
            num_scalar_prefetch=1,
            grid=(steps,),
            in_specs=[
                pl.BlockSpec((lists, step), lambda b, base: (0, b)),
                pl.BlockSpec((step, lists * width), lambda b, base: (b, 0)),
            ],
            out_specs=pl.BlockSpec((kept, lists * width), lambda b, base: (0, 0)),
            scratch_shapes=[pltpu.VMEM((kept + sub + 16, lists * width), jnp.float32)],
        ),
        compiler_params=pltpu.CompilerParams(dimension_semantics=("arbitrary",)),
    )(base, pos, source)


def make_body(n_row, n_col):
    def body(amplitudes, integrals, pair_label, orbital_irrep, column_label):
        pair_rows, cd_count = amplitudes.shape
        orb_width = orbital_irrep.shape[0]
        c_count = cd_count // orb_width
        ab_count = integrals.shape[1]
        col_i = lax.axis_index("col")
        row_i = lax.axis_index("row")
        c_irrep = lax.dynamic_slice_in_dim(orbital_irrep, col_i * c_count, c_count)
        cd_label = jnp.bitwise_xor(c_irrep[:, None], orbital_irrep[None, :]).reshape(cd_count)
        row_label = jnp.repeat(pair_label, pair_rows // pair_label.shape[0])

        def dense(_):
            int_cube = integrals.reshape(c_count, orb_width, ab_count)
            swapped = lax.all_to_all(int_cube, "col", split_axis=1, concat_axis=0, tiled=True)
            mirrored = jnp.transpose(swapped, (1, 0, 2)).reshape(cd_count, ab_count)
            ab_label = jnp.repeat(column_label, PAIR_BLOCK)
            amp_keep = row_label[:, None] == cd_label[None, :]
            slab_keep = cd_label[:, None] == ab_label[None, :]
            amp_kept = jnp.where(amp_keep, amplitudes, jnp.zeros_like(amplitudes))
            int_slab = lax.all_gather(integrals, "row", axis=1, tiled=True)
            mirror_slab = lax.all_gather(mirrored, "row", axis=1, tiled=True)
            int_kept = jnp.where(slab_keep, int_slab, jnp.zeros_like(int_slab))
            mirror_kept = jnp.where(slab_keep, mirror_slab, jnp.zeros_like(mirror_slab))
            direct = jnp.einsum("ka,pk->ap", int_kept, amp_kept, preferred_element_type=jnp.float32)
            crossed = jnp.einsum("ka,pk->ap", mirror_kept, amp_kept, preferred_element_type=jnp.float32)
            return direct - crossed

        single = ab_count <= PAIR_BLOCK and PAIR_BLOCK % ab_count == 0
        if not single:
            partial = dense(None)
        else:
            block_label = column_label[(jnp.arange(n_row) * ab_count) // PAIR_BLOCK]
            irreps = jnp.arange(IRREPS, dtype=orbital_irrep.dtype)
            blk_irrep = orbital_irrep.reshape(n_col, c_count)
            blk_cnt = jnp.sum(blk_irrep[:, :, None] == irreps[None, None, :], axis=1)
            xor_tab = jnp.bitwise_xor(irreps[:, None], irreps[None, :])
            pair_cnt = jnp.einsum("ak,bkl->abl", blk_cnt, blk_cnt[:, xor_tab])
            largest = jnp.max(pair_cnt[:, :, block_label])
            pair_cells = c_count * c_count
            caps = [t * pair_cells // 32 for t in TIERS]
            tier = sum((largest > cap).astype(jnp.int32) for cap in caps)
            own_irrep = blk_irrep[col_i]
            n_pb = pair_label.shape[0]
            pb = pair_rows // n_pb

            lab_jdc = jnp.bitwise_xor(blk_irrep[:, :, None], own_irrep[None, None, :])
            lab_bcd = jnp.bitwise_xor(own_irrep[None, :, None], blk_irrep[:, None, :])
            p_lab = pair_label.astype(lab_jdc.dtype)

            def compact(cap):
                def run(_):
                    int_jdc = jnp.transpose(integrals.reshape(c_count, n_col, c_count, ab_count), (1, 2, 0, 3))
                    int_jdc = int_jdc.reshape(cd_count, ab_count)
                    sent = compact_rows(
                        int_jdc, (lab_jdc == block_label[row_i])[None], pair_cells, cap, 1, ab_count
                    )
                    got = lax.all_gather(sent, "row", axis=0, tiled=False)
                    amp_jcd = jnp.transpose(amplitudes.reshape(pair_rows, c_count, n_col, c_count), (2, 1, 3, 0))
                    amp_jcd = amp_jcd.reshape(cd_count, pair_rows)
                    amp_dc = jnp.transpose(amplitudes.reshape(pair_rows, c_count, orb_width), (2, 1, 0))
                    amp_dc = amp_dc.reshape(cd_count, pair_rows)
                    outgoing = compact_rows(
                        amp_jcd, lab_bcd[None] == p_lab[:, None, None, None], pair_cells, cap, n_pb, pb
                    )
                    incoming = lax.all_to_all(outgoing, "col", split_axis=0, concat_axis=0, tiled=True)
                    direct = compact_rows(
                        amp_dc, lab_jdc[None] == p_lab[:, None, None, None], pair_cells, cap, n_pb, pb
                    )
                    both = jnp.concatenate([direct, incoming], axis=1)
                    prod = jnp.einsum("imq,mx->iqx", got, both, preferred_element_type=jnp.float32)
                    diff = prod[..., :pair_rows] - prod[..., pair_rows:]
                    keep = block_label[:, None] == row_label[None, :]
                    diff = jnp.where(keep[:, None, :], diff, jnp.zeros_like(diff))
                    return diff.reshape(n_row * ab_count, pair_rows)

                return run

            branches = [compact(cap) for cap in caps] + [dense]
            partial = lax.switch(tier, branches, None)
        parts = lax.all_to_all(
            partial.reshape(n_col, partial.shape[0] // n_col, pair_rows), "col", split_axis=0, concat_axis=0, tiled=True
        )
        return jnp.sum(parts, axis=0).astype(jnp.bfloat16)

    return body


def solution(mesh):
    placed = (P("row", "col"), P("col", "row"), P("row"), P(), P())
    return jax.shard_map(
        make_body(mesh.shape["row"], mesh.shape["col"]),
        mesh=mesh,
        in_specs=placed,
        out_specs=P("col", "row"),
        check_vma=False,
    )
```
